256 devices in a mesh: circ: 8 (over y_lo, x), span: 32 (over y_hi, z, core).
Axes of the slice: x: 4, y: 4 (y_hi: 2, y_lo: 2; y = y_hi * 2 + y_lo), z: 8, core: 2. Of those that a mesh axis runs over, the one named last changes fastest.
Arguments:
- q_old: float32 [5, 32, 4096, 128], P(None, 'circ', 'span'), may hold values from -6 to 6
- pseudo_rate: float32 [32, 4096, 128], P('circ', 'span'), may hold values from 0.15 to 0.45
- flux_jacobians: float32 [3, 5, 5], replicated, may hold values from -2.5 to 2.5
- rotor_face: float32 [5, 32, 4096], P(None, 'circ', 'span'), may hold values from -6 to 6
- offsets: int32 [4096], P('span'), may hold values from 0 to 31
- owners: int32 [8, 128, 4], P('circ', 'span'), may hold values from 0 to 31, all different within a row; in each aligned block of 4 rows (0 to 3, 4 to 7, ..., all dimensions but the last counted through in order) at most 2 rows name the same one
- slots: int32 [8, 128, 4], P('circ', 'span'), may hold values from 0 to 3
- weight_idx: int32 [8, 128, 4], P('circ', 'span'), may hold values from 0 to 15
- weight_table: float32 [16], replicated, may hold values from 0.3 to 1
Outputs:
- q_new: float32 [5, 32, 4096, 128], P(None, 'circ', 'span')
The draws below stay inside these ranges and needn't reach their ends.
Inputs may be any that keep to these rules, and one draw needn't show every extreme that they name: The 4 owners of one rotor panel differ; among the 4 rotor panels of one device in one circumferential block, no owner is named more than 2 times, and that count is reached.
All inputs are finite; a program needn't handle non-finite values.
Results may differ from the reference program's by a relative error of at most 0.000068.
Values sent between devices are 32-bit elements; how exact they have to be, the bound alone decides.
No kernel may reach another device: no remote copies, remote signals or barrier semaphores. Data moves between devices by JAX's collectives and lax.ppermute only.
A program may use at most 64 MiB of HBM per device.

```python
import math
import jax
import jax.numpy as jnp
import numpy as np
from jax import lax

NF = 5
CT = 4
KP_DEV = 4
PW = 32
TOP = 4
NW = 16
CA = 128
CAP = 2
NB = 8
NT = 32
NS = 4096
KP = 128
N_SPAN = 32


def with_ends(drawn, stream_key, least, largest):
    longest = drawn.shape.index(max(drawn.shape))
    spots = []
    for shift in (0, 1):
        where = [jax.random.randint(jax.random.fold_in(stream_key, axis), (), 0, length) for axis, length in enumerate(drawn.shape)]
        where[longest] = (where[longest] + shift) % drawn.shape[longest]
        spots.append(tuple(where))
    return drawn.at[spots[0]].set(least).at[spots[1]].set(largest)


def block_scale(stream_key, extent, pieces, least, high):
    def one(dim, shards_of):
        heights = jax.random.uniform(jax.random.fold_in(jax.random.fold_in(stream_key, 6), dim), (shards_of,), jnp.float32, least / len(pieces), high / len(pieces))
        return jnp.repeat(jnp.exp(heights), extent[dim] // shards_of).reshape((-1,) + (1,) * (len(extent) - dim - 1))

    loudness = one(*pieces[0])
    for cut in pieces[1:]:
        loudness = loudness * one(*cut)
    return loudness


def shared_out(key, own, number, rows, count, top, limit, lean):
    order = jax.random.permutation(key, count)
    packed, usual = portions_of(count, rows * top, limit, lean, True), portions_of(count, rows * top, limit, lean, False)
    places = jnp.arange(count)

    def named(lengths, offset_by):
        used = int((lengths > 0).sum())
        fixed = max(1, used // 4)
        shifted = fixed + (places - fixed + offset_by * (used - fixed)) % max(1, count - fixed)
        return jnp.zeros((count,), jnp.int32).at[order[jnp.where(places < fixed, places, shifted)]].set(jnp.asarray(lengths, jnp.int32))

    lengths = jnp.where(number % 4 == 0, named(packed, number // 4), named(usual, number - number // 4 - 1))
    mixed = jax.random.permutation(jax.random.fold_in(own, 3), count)
    giver, receiver = mixed[0:count // 2 * 2:2], mixed[1:count // 2 * 2:2]
    slack = jnp.minimum(lengths[giver] - 1, limit - lengths[receiver]) // 2
    slack = jnp.where((giver == order[0]) | (receiver == order[0]) | (lengths[receiver] == 0), 0, jnp.maximum(slack, 0))
    shifted = jax.random.randint(jax.random.fold_in(own, 4), (count // 2,), 0, 1 << 20) % (slack + 1)
    lengths = lengths.at[giver].add(-shifted).at[receiver].add(shifted)
    items = jnp.searchsorted(jnp.cumsum(lengths), jnp.arange(rows * top), side="right").astype(jnp.int32)
    table = items.reshape(top, rows).T
    table = table[jax.random.permutation(jax.random.fold_in(own, 1), rows)]
    offset_by = jax.random.randint(jax.random.fold_in(own, 2), (rows, 1), 0, top)
    return jnp.take_along_axis(table, (jnp.arange(top)[None, :] + offset_by) % top, axis=1)


def portions_of(count, total, limit, lean, full):
    loads = [(1 << 20) // math.isqrt(grade ** lean) + 1 for grade in range(1, count + 1)]
    largest = limit if full else min(limit, max(-(-total // count), total * loads[0] // sum(loads)))
    least = 1 if total - largest >= count - 1 else 0
    counts, spare = [largest] + [least] * (count - 1), total - largest - least * (count - 1)
    while spare > 0:
        free = [i for i in range(1, count) if counts[i] < largest] or [i for i in range(1, count) if counts[i] < limit]
        pool, left = sum([loads[i] for i in free]), spare
        for i in free:
            extra = min(limit - counts[i], max(1, left * loads[i] // pool), spare)
            counts[i] = counts[i] + extra
            spare = spare - extra
    return np.array(counts)


def centred(rng, extent, deviation, bound, cuts=(), kind=jnp.bfloat16):
    entries = deviation * jax.random.normal(rng, extent, jnp.float32)
    if cuts:
        entries = entries * block_scale(rng, extent, cuts, -0.22, 0.18)
    return jnp.clip(entries, -bound, bound).astype(kind)


def setup_inputs(seed: int = 0) -> dict:
    key_list = jax.random.split(jax.random.key(seed), 10)
    q_old = centred(key_list[0], (NF, NT, NS, CA), 1.0, 6.0, ((1, 8), (2, 32)), jnp.float32)
    pseudo_rate = jnp.clip(jnp.exp(math.log(0.45) - 1.0986122 * jax.random.uniform(key_list[1], (NT, NS, CA), jnp.float32) ** block_scale(key_list[1], (NT, NS, CA), ((0, 8), (1, 32)), -0.2, 0.2)), 0.15, 0.45)
    flux_jacobians = centred(key_list[2], (3, NF, NF), NF ** -0.5, 2.5, (), jnp.float32)
    rotor_face = centred(key_list[3], (NF, NT, NS), 1.0, 6.0, ((1, 8), (2, 32)), jnp.float32)
    offsets = with_ends(jax.random.randint(key_list[4], (NS,), 0, NT), jax.random.fold_in(key_list[4], 1), 0, NT - 1).astype(jnp.int32)
    owners_keys = jax.random.split(jax.random.fold_in(key_list[5], 1), NB * KP // KP_DEV)
    owners_turns = jax.random.permutation(jax.random.fold_in(key_list[5], 3), NB * KP // KP_DEV)
    owners = jax.vmap(lambda own, number: shared_out(jax.random.fold_in(key_list[5], 2), own, number, KP_DEV, N_SPAN, TOP, CAP, 2))(owners_keys, owners_turns).reshape((NB, KP, TOP))
    slots = with_ends(jax.random.randint(key_list[6], (NB, KP, TOP), 0, KP_DEV), jax.random.fold_in(key_list[6], 1), 0, KP_DEV - 1).astype(jnp.int32)
    weight_idx = with_ends(jax.random.randint(key_list[7], (NB, KP, TOP), 0, NW), jax.random.fold_in(key_list[7], 1), 0, NW - 1).astype(jnp.int32)
    weight_table = jnp.clip(jax.random.uniform(key_list[8], (NW,), jnp.float32, 0.3, 1.0), 0.3, 1.0)
    return {"q_old": q_old, "pseudo_rate": pseudo_rate, "flux_jacobians": flux_jacobians, "rotor_face": rotor_face, "offsets": offsets, "owners": owners, "slots": slots, "weight_idx": weight_idx, "weight_table": weight_table}


inv_step = 0.5
viscosity = 0.1


def contract(matrix, values):
    return jnp.einsum("fg,gtsa->ftsa", matrix, values, precision=lax.Precision.HIGHEST)


def advance(padded, current, previous, rate_cells, inlet_plane, jacobians):
    circ_up = padded[:, 2:, 1:-1]
    circ_down = padded[:, :-2, 1:-1]
    span_up = padded[:, 1:-1, 2:]
    span_down = padded[:, 1:-1, :-2]
    zero_column = jnp.zeros_like(current[..., :1])
    axial_up = jnp.concatenate([current[..., 1:], zero_column], axis=-1)
    axial_down = jnp.concatenate([inlet_plane[..., None], current[..., :-1]], axis=-1)
    convection = contract(jacobians[0], circ_up - circ_down)
    convection = convection + contract(jacobians[1], span_up - span_down)
    convection = convection + contract(jacobians[2], axial_up - axial_down)
    laplacian = (circ_up + circ_down) + (span_up + span_down) + (axial_up + axial_down) - 6.0 * current
    residual = inv_step * (current - previous) + 0.5 * convection - viscosity * laplacian
    return current - rate_cells[None] * residual


def extend(field_values):
    wrapped = jnp.concatenate([field_values[:, -1:], field_values, field_values[:, :1]], axis=1)
    return jnp.pad(wrapped, ((0, 0), (0, 0), (1, 1), (0, 0)))


def reference(q_old, pseudo_rate, flux_jacobians, rotor_face, offsets, owners, slots, weight_idx, weight_table):
    source_rows = (jnp.arange(NT, dtype=jnp.int32)[:, None] - offsets[None, :]) % NT
    rotated = jnp.take_along_axis(rotor_face, source_rows[None].astype(jnp.int32), axis=1)
    panels = rotated.reshape(NF, NB, CT, KP, PW)
    weights = weight_table[weight_idx]
    targets = owners * KP_DEV + slots
    panel_ids = jnp.arange(KP, dtype=jnp.int32)
    mixing = jnp.sum(jnp.where(targets[:, None, :, :] == panel_ids[None, :, None, None], weights[:, None, :, :], 0.0), axis=-1)
    inlet_plane = jnp.einsum("cgk,fctkp->fctgp", mixing, panels, precision=lax.Precision.HIGHEST).reshape(NF, NT, NS)
    first_pass = advance(extend(q_old), q_old, q_old, pseudo_rate, inlet_plane, flux_jacobians)
    return advance(extend(first_pass), first_pass, q_old, pseudo_rate, inlet_plane, flux_jacobians)
```

```python
import jax
import jax.numpy as jnp
from jax import lax
from jax.sharding import PartitionSpec as P

NF = 5
KP_DEV = 4
PW = 32


inv_step = 0.5
viscosity = 0.1


def with_halo(block, sides, width):
    for axis, dim in sides:
        count = lax.axis_size(axis)
        forward = [(i, i + 1) for i in range(count - 1)]
        forward.append((count - 1, 0))
        backward = [(target, source) for source, target in forward]
        low = lax.ppermute(
            lax.slice_in_dim(block, block.shape[dim] - width, None, axis=dim), axis, forward
        )
        high = lax.ppermute(lax.slice_in_dim(block, 0, width, axis=dim), axis, backward)
        block = jnp.concatenate([low, block, high], axis=dim)
    return block


def contract(matrix, values):
    return jnp.einsum("fg,gtsa->ftsa", matrix, values, precision=lax.Precision.HIGHEST)


def advance(padded, current, previous, rate_cells, inlet_plane, jacobians):
    circ_up = padded[:, 2:, 1:-1]
    circ_down = padded[:, :-2, 1:-1]
    span_up = padded[:, 1:-1, 2:]
    span_down = padded[:, 1:-1, :-2]
    zero_column = jnp.zeros_like(current[..., :1])
    axial_up = jnp.concatenate([current[..., 1:], zero_column], axis=-1)
    axial_down = jnp.concatenate([inlet_plane[..., None], current[..., :-1]], axis=-1)
    convection = contract(jacobians[0], circ_up - circ_down)
    convection = convection + contract(jacobians[1], span_up - span_down)
    convection = convection + contract(jacobians[2], axial_up - axial_down)
    laplacian = (
        circ_up + circ_down + (span_up + span_down) + (axial_up + axial_down) - 6.0 * current
    )
    residual = inv_step * (current - previous) + 0.5 * convection - viscosity * laplacian
    return current - rate_cells[None] * residual


def wall_zero(field_array, width):
    span_index = lax.axis_index("span")
    span_count = lax.axis_size("span")
    length = field_array.shape[2]
    position = jnp.arange(length, dtype=jnp.int32)
    at_hub = jnp.logical_and(span_index == 0, position < width)
    at_tip = jnp.logical_and(span_index == span_count - 1, position >= length - width)
    keeping = jnp.logical_not(jnp.logical_or(at_hub, at_tip)).astype(field_array.dtype)
    keeping = keeping.reshape(1, 1, length, 1)
    return field_array * keeping


def body(
    q_old, pseudo_rate, flux_jacobians, rotor_face, offsets, owners, slots, weight_idx, weight_table
):
    circ_count = lax.axis_size("circ")
    rows_local = rotor_face.shape[1]
    total_rows = rows_local * circ_count
    row_iota = jnp.arange(rows_local, dtype=jnp.int32)
    all_rows = lax.all_gather(rotor_face, "circ", axis=1, tiled=True)
    first_row = lax.axis_index("circ") * rows_local
    source_rows = (first_row + row_iota[:, None] - offsets[None, :]) % total_rows
    rotated = jnp.take_along_axis(all_rows, source_rows[None], axis=1)
    panels = rotated.reshape(NF, rows_local, KP_DEV, PW)
    table_ids = jnp.arange(weight_table.shape[0], dtype=jnp.int32)
    weights = jnp.sum(jnp.where(weight_idx[..., None] == table_ids, weight_table, 0.0), axis=-1)
    targets = owners[0] * KP_DEV + slots[0]
    local_weights = weights[0]
    panel_ids = jnp.arange(KP_DEV * lax.axis_size("span"), dtype=jnp.int32)
    mixing = jnp.sum(
        jnp.where(targets[None] == panel_ids[:, None, None], local_weights[None], 0.0), axis=-1
    )
    span_count = lax.axis_size("span")
    contributions = jnp.einsum("gk,ftkp->gftp", mixing, panels, precision=lax.Precision.HIGHEST)
    contributions = contributions.reshape((span_count, KP_DEV) + contributions.shape[1:])
    received = lax.all_to_all(contributions, "span", 0, 0, tiled=True)
    own_panels = jnp.sum(received, axis=0)
    inlet_plane = jnp.transpose(own_panels, (1, 2, 0, 3)).reshape(NF, rows_local, KP_DEV * PW)

    def sweep(current):
        padded = with_halo(current, (("circ", 1), ("span", 2)), 1)
        padded = wall_zero(padded, 1)
        return advance(padded, current, q_old, pseudo_rate, inlet_plane, flux_jacobians)

    first_pass = sweep(q_old)
    return sweep(first_pass)


def solution(mesh):
    return jax.shard_map(
        body,
        mesh=mesh,
        in_specs=(
            P(None, "circ", "span", None),
            P("circ", "span", None),
            P(),
            P(None, "circ", "span"),
            P("span"),
            P("circ", "span", None),
            P("circ", "span", None),
            P("circ", "span", None),
            P(),
        ),
        out_specs=P(None, "circ", "span", None),
        check_vma=False,
    )
```

```python
import jax
import jax.numpy as jnp
from jax import lax
from jax.sharding import PartitionSpec as P

NF = 5
KP_DEV = 4
PW = 32


inv_step = 0.5
viscosity = 0.1


def with_halo(block, sides, width):
    for axis, dim in sides:
        count = lax.axis_size(axis)
        forward = [(i, i + 1) for i in range(count - 1)]
        forward.append((count - 1, 0))
        backward = [(target, source) for source, target in forward]
        low = lax.ppermute(
            lax.slice_in_dim(block, block.shape[dim] - width, None, axis=dim), axis, forward
        )
        high = lax.ppermute(lax.slice_in_dim(block, 0, width, axis=dim), axis, backward)
        block = jnp.concatenate([low, block, high], axis=dim)
    return block


def contract(matrix, values):
    total = matrix[:, 0, None, None, None] * values[0][None]
    for g in range(1, matrix.shape[1]):
        total = total + matrix[:, g, None, None, None] * values[g][None]
    return total


def update(current, previous, rate_cells, neighbours, jacobians):
    circ_up, circ_down, span_up, span_down, axial_up, axial_down = neighbours
    convection = contract(jacobians[0], circ_up - circ_down)
    convection = convection + contract(jacobians[1], span_up - span_down)
    convection = convection + contract(jacobians[2], axial_up - axial_down)
    laplacian = (
        circ_up + circ_down + (span_up + span_down) + (axial_up + axial_down) - 6.0 * current
    )
    residual = inv_step * (current - previous) + 0.5 * convection - viscosity * laplacian
    return current - rate_cells[None] * residual


def lateral(padded):
    return (
        padded[:, 2:, 1:-1],
        padded[:, :-2, 1:-1],
        padded[:, 1:-1, 2:],
        padded[:, 1:-1, :-2],
    )


def advance(padded, current, previous, rate_cells, jacobians):
    zero_column = jnp.zeros_like(current[..., :1])
    axial_up = jnp.concatenate([current[..., 1:], zero_column], axis=-1)
    axial_down = jnp.concatenate([zero_column, current[..., :-1]], axis=-1)
    neighbours = lateral(padded) + (axial_up, axial_down)
    return update(current, previous, rate_cells, neighbours, jacobians)


def wall_zero(field_array, width):
    span_index = lax.axis_index("span")
    span_count = lax.axis_size("span")
    length = field_array.shape[2]
    position = jnp.arange(length, dtype=jnp.int32)
    at_hub = jnp.logical_and(span_index == 0, position < width)
    at_tip = jnp.logical_and(span_index == span_count - 1, position >= length - width)
    keeping = jnp.logical_not(jnp.logical_or(at_hub, at_tip)).astype(field_array.dtype)
    keeping = keeping.reshape(1, 1, length, 1)
    return field_array * keeping


def body(
    q_old, pseudo_rate, flux_jacobians, rotor_face, offsets, owners, slots, weight_idx, weight_table
):
    circ_count = lax.axis_size("circ")
    rows_local = rotor_face.shape[1]
    total_rows = rows_local * circ_count
    row_iota = jnp.arange(rows_local, dtype=jnp.int32)
    copies = jnp.broadcast_to(rotor_face[None], (circ_count,) + rotor_face.shape)
    gathered = lax.all_to_all(copies, "circ", 0, 0, tiled=True)
    all_rows = jnp.transpose(gathered, (1, 0, 2, 3)).reshape(NF, total_rows, rotor_face.shape[2])
    first_row = lax.axis_index("circ") * rows_local
    source_rows = (first_row + row_iota[:, None] - offsets[None, :]) % total_rows
    rotated = jnp.take_along_axis(all_rows, source_rows[None], axis=1)
    panels = rotated.reshape(NF, rows_local, KP_DEV, PW)
    table_ids = jnp.arange(weight_table.shape[0], dtype=jnp.int32)
    weights = jnp.sum(jnp.where(weight_idx[..., None] == table_ids, weight_table, 0.0), axis=-1)
    targets = owners[0] * KP_DEV + slots[0]
    local_weights = weights[0]
    panel_ids = jnp.arange(KP_DEV * lax.axis_size("span"), dtype=jnp.int32)
    mixing = jnp.sum(
        jnp.where(targets[None] == panel_ids[:, None, None], local_weights[None], 0.0), axis=-1
    )
    span_count = lax.axis_size("span")
    contributions = jnp.einsum("gk,ftkp->gftp", mixing, panels, precision=lax.Precision.HIGHEST)
    contributions = contributions.reshape((span_count, KP_DEV) + contributions.shape[1:])
    received = lax.all_to_all(contributions, "span", 0, 0, tiled=True)
    own_panels = jnp.sum(received, axis=0)
    inlet_plane = jnp.transpose(own_panels, (1, 2, 0, 3)).reshape(NF, rows_local, KP_DEV * PW)

    def padded_of(current):
        return wall_zero(with_halo(current, (("circ", 1), ("span", 2)), 1), 1)

    padded_old = padded_of(q_old)
    mid_bulk = advance(padded_old, q_old, q_old, pseudo_rate, flux_jacobians)
    padded_mid = padded_of(mid_bulk)
    new_bulk = advance(padded_mid, mid_bulk, q_old, pseudo_rate, flux_jacobians)

    inlet = inlet_plane[..., None]
    old_edge = lateral(padded_old[..., :1]) + (q_old[..., 1:2], inlet)
    mid_first = update(
        q_old[..., :1], q_old[..., :1], pseudo_rate[..., :1], old_edge, flux_jacobians
    )
    mid_pair = jnp.concatenate([mid_first, mid_bulk[..., 1:2]], axis=-1)
    mid_edge = lateral(padded_of(mid_pair)) + (
        mid_bulk[..., 1:3],
        jnp.concatenate([inlet, mid_first], axis=-1),
    )
    new_pair = update(mid_pair, q_old[..., :2], pseudo_rate[..., :2], mid_edge, flux_jacobians)
    return jnp.concatenate([new_pair, new_bulk[..., 2:]], axis=-1)


def solution(mesh):
    return jax.shard_map(
        body,
        mesh=mesh,
        in_specs=(
            P(None, "circ", "span", None),
            P("circ", "span", None),
            P(),
            P(None, "circ", "span"),
            P("span"),
            P("circ", "span", None),
            P("circ", "span", None),
            P("circ", "span", None),
            P(),
        ),
        out_specs=P(None, "circ", "span", None),
        check_vma=False,
    )
```

```python
import jax
import jax.numpy as jnp
from jax import lax
from jax.experimental import pallas as pl
from jax.experimental.pallas import tpu as pltpu
from jax.sharding import PartitionSpec as P

NF = 5
KP_DEV = 4
PW = 32


inv_step = 0.5
viscosity = 0.1


def with_halo(block, sides, width):
    for axis, dim in sides:
        count = lax.axis_size(axis)
        forward = [(i, i + 1) for i in range(count - 1)]
        forward.append((count - 1, 0))
        backward = [(target, source) for source, target in forward]
        low = lax.ppermute(
            lax.slice_in_dim(block, block.shape[dim] - width, None, axis=dim), axis, forward
        )
        high = lax.ppermute(lax.slice_in_dim(block, 0, width, axis=dim), axis, backward)
        block = jnp.concatenate([low, block, high], axis=dim)
    return block


def halo_parts(block):
    parts = []
    for axis, dim in (("circ", 1), ("span", 2)):
        count = lax.axis_size(axis)
        forward = [(i, (i + 1) % count) for i in range(count)]
        backward = [(target, source) for source, target in forward]
        low = lax.ppermute(lax.slice_in_dim(block, block.shape[dim] - 1, None, axis=dim), axis, forward)
        high = lax.ppermute(lax.slice_in_dim(block, 0, 1, axis=dim), axis, backward)
        parts += [low, high]
    span_index = lax.axis_index("span")
    span_last = lax.axis_size("span") - 1
    parts[2] = parts[2] * (span_index != 0).astype(block.dtype)
    parts[3] = parts[3] * (span_index != span_last).astype(block.dtype)
    return parts


def lateral_of(block, parts):
    circ_low, circ_high, span_low, span_high = parts
    return (
        jnp.concatenate([block[:, 1:], circ_high], axis=1),
        jnp.concatenate([circ_low, block[:, :-1]], axis=1),
        jnp.concatenate([block[:, :, 1:], span_high], axis=2),
        jnp.concatenate([span_low, block[:, :, :-1]], axis=2),
    )


def stencil_kernel(j_ref, c_ref, cu_ref, cd_ref, su_ref, sd_ref, prev_ref, rate_ref, out_ref):
    lane = lax.broadcasted_iota(jnp.int32, (8, 128), 1)
    probe = pltpu.roll(lane, 1, 1)
    numpy_order = probe == (lane + 127) % 128

    def chunk(i, carry):
        rows = pl.ds(pl.multiple_of(i * 8, 8), 8)
        cur = [c_ref[g, 0, rows, :] for g in range(NF)]
        cu = [cu_ref[g, 0, rows, :] for g in range(NF)]
        cd = [cd_ref[g, 0, rows, :] for g in range(NF)]
        su = [su_ref[g, 0, rows, :] for g in range(NF)]
        sd = [sd_ref[g, 0, rows, :] for g in range(NF)]
        au, ad = [], []
        for g in range(NF):
            one = pltpu.roll(cur[g], 1, 1)
            other = pltpu.roll(cur[g], 127, 1)
            down = jnp.where(numpy_order, one, other)
            up = jnp.where(numpy_order, other, one)
            ad.append(jnp.where(lane == 0, 0.0, down))
            au.append(jnp.where(lane == 127, 0.0, up))
        dc = [cu[g] - cd[g] for g in range(NF)]
        ds = [su[g] - sd[g] for g in range(NF)]
        da = [au[g] - ad[g] for g in range(NF)]
        rate = rate_ref[0, rows, :]
        for f in range(NF):
            convection = None
            for d, diff in enumerate((dc, ds, da)):
                term = j_ref[d * NF * NF + f * NF] * diff[0]
                for g in range(1, NF):
                    term = term + j_ref[d * NF * NF + f * NF + g] * diff[g]
                convection = term if convection is None else convection + term
            laplacian = cu[f] + cd[f] + (su[f] + sd[f]) + (au[f] + ad[f]) - 6.0 * cur[f]
            residual = (
                inv_step * (cur[f] - prev_ref[f, 0, rows, :])
                + 0.5 * convection
                - viscosity * laplacian
            )
            out_ref[f, 0, rows, :] = cur[f] - rate * residual
        return carry

    lax.fori_loop(0, c_ref.shape[2] // 8, chunk, 0)


def bulk_sweep(current, previous, rate_cells, jacobians):
    parts = halo_parts(current)
    circ_low, circ_high, span_low, span_high = parts
    padded = jnp.concatenate([circ_low, current, circ_high], axis=1)
    span_up = jnp.concatenate([current[:, :, 1:], span_high], axis=2)
    span_down = jnp.concatenate([span_low, current[:, :, :-1]], axis=2)
    nf, rows, span, axial = current.shape
    block = (nf, 1, span, axial)
    spec = lambda shift: pl.BlockSpec(block, lambda t: (0, t + shift, 0, 0))
    out = pl.pallas_call(
        stencil_kernel,
        grid=(rows,),
        in_specs=[
            pl.BlockSpec(memory_space=pltpu.SMEM),
            spec(1),
            spec(2),
            spec(0),
            spec(0),
            spec(0),
            spec(0),
            pl.BlockSpec((1, span, axial), lambda t: (t, 0, 0)),
        ],
        out_specs=spec(0),
        out_shape=jax.ShapeDtypeStruct(current.shape, current.dtype),
    )(jacobians.reshape(-1), padded, padded, padded, span_up, span_down, previous, rate_cells)
    return out, parts


def contract(matrix, values):
    total = matrix[:, 0, None, None, None] * values[0][None]
    for g in range(1, matrix.shape[1]):
        total = total + matrix[:, g, None, None, None] * values[g][None]
    return total


def update(current, previous, rate_cells, neighbours, jacobians):
    circ_up, circ_down, span_up, span_down, axial_up, axial_down = neighbours
    convection = contract(jacobians[0], circ_up - circ_down)
    convection = convection + contract(jacobians[1], span_up - span_down)
    convection = convection + contract(jacobians[2], axial_up - axial_down)
    laplacian = (
        circ_up + circ_down + (span_up + span_down) + (axial_up + axial_down) - 6.0 * current
    )
    residual = inv_step * (current - previous) + 0.5 * convection - viscosity * laplacian
    return current - rate_cells[None] * residual


def lateral(padded):
    return (
        padded[:, 2:, 1:-1],
        padded[:, :-2, 1:-1],
        padded[:, 1:-1, 2:],
        padded[:, 1:-1, :-2],
    )


def advance(padded, current, previous, rate_cells, jacobians):
    zero_column = jnp.zeros_like(current[..., :1])
    axial_up = jnp.concatenate([current[..., 1:], zero_column], axis=-1)
    axial_down = jnp.concatenate([zero_column, current[..., :-1]], axis=-1)
    neighbours = lateral(padded) + (axial_up, axial_down)
    return update(current, previous, rate_cells, neighbours, jacobians)


def wall_zero(field_array, width):
    span_index = lax.axis_index("span")
    span_count = lax.axis_size("span")
    length = field_array.shape[2]
    position = jnp.arange(length, dtype=jnp.int32)
    at_hub = jnp.logical_and(span_index == 0, position < width)
    at_tip = jnp.logical_and(span_index == span_count - 1, position >= length - width)
    keeping = jnp.logical_not(jnp.logical_or(at_hub, at_tip)).astype(field_array.dtype)
    keeping = keeping.reshape(1, 1, length, 1)
    return field_array * keeping


def body(
    q_old, pseudo_rate, flux_jacobians, rotor_face, offsets, owners, slots, weight_idx, weight_table
):
    circ_count = lax.axis_size("circ")
    rows_local = rotor_face.shape[1]
    total_rows = rows_local * circ_count
    row_iota = jnp.arange(rows_local, dtype=jnp.int32)
    copies = jnp.broadcast_to(rotor_face[None], (circ_count,) + rotor_face.shape)
    gathered = lax.all_to_all(copies, "circ", 0, 0, tiled=True)
    all_rows = jnp.transpose(gathered, (1, 0, 2, 3)).reshape(NF, total_rows, rotor_face.shape[2])
    first_row = lax.axis_index("circ") * rows_local
    source_rows = (first_row + row_iota[:, None] - offsets[None, :]) % total_rows
    rotated = jnp.take_along_axis(all_rows, source_rows[None], axis=1)
    panels = rotated.reshape(NF, rows_local, KP_DEV, PW)
    table_ids = jnp.arange(weight_table.shape[0], dtype=jnp.int32)
    weights = jnp.sum(jnp.where(weight_idx[..., None] == table_ids, weight_table, 0.0), axis=-1)
    targets = owners[0] * KP_DEV + slots[0]
    local_weights = weights[0]
    panel_ids = jnp.arange(KP_DEV * lax.axis_size("span"), dtype=jnp.int32)
    mixing = jnp.sum(
        jnp.where(targets[None] == panel_ids[:, None, None], local_weights[None], 0.0), axis=-1
    )
    span_count = lax.axis_size("span")
    contributions = jnp.einsum("gk,ftkp->gftp", mixing, panels, precision=lax.Precision.HIGHEST)
    contributions = contributions.reshape((span_count, KP_DEV) + contributions.shape[1:])
    received = lax.all_to_all(contributions, "span", 0, 0, tiled=True)
    own_panels = jnp.sum(received, axis=0)
    inlet_plane = jnp.transpose(own_panels, (1, 2, 0, 3)).reshape(NF, rows_local, KP_DEV * PW)

    mid_bulk, old_parts = bulk_sweep(q_old, q_old, pseudo_rate, flux_jacobians)
    new_bulk, mid_parts = bulk_sweep(mid_bulk, q_old, pseudo_rate, flux_jacobians)

    inlet = inlet_plane[..., None]
    old_edge = lateral_of(q_old[..., :1], [p[..., :1] for p in old_parts]) + (
        q_old[..., 1:2],
        inlet,
    )
    mid_first = update(
        q_old[..., :1], q_old[..., :1], pseudo_rate[..., :1], old_edge, flux_jacobians
    )
    mid_pair = jnp.concatenate([mid_first, mid_bulk[..., 1:2]], axis=-1)
    mid_edge = lateral_of(mid_pair, halo_parts(mid_pair)) + (
        mid_bulk[..., 1:3],
        jnp.concatenate([inlet, mid_first], axis=-1),
    )
    new_pair = update(mid_pair, q_old[..., :2], pseudo_rate[..., :2], mid_edge, flux_jacobians)
    return jnp.concatenate([new_pair, new_bulk[..., 2:]], axis=-1)


def solution(mesh):
    return jax.shard_map(
        body,
        mesh=mesh,
        in_specs=(
            P(None, "circ", "span", None),
            P("circ", "span", None),
            P(),
            P(None, "circ", "span"),
            P("span"),
            P("circ", "span", None),
            P("circ", "span", None),
            P("circ", "span", None),
            P(),
        ),
        out_specs=P(None, "circ", "span", None),
        check_vma=False,
    )
```

```python
import jax
import jax.numpy as jnp
from jax import lax
from jax.experimental import pallas as pl
from jax.experimental.pallas import tpu as pltpu
from jax.sharding import PartitionSpec as P

NF = 5
KP_DEV = 4
PW = 32


inv_step = 0.5
viscosity = 0.1


def with_halo(block, sides, width):
    for axis, dim in sides:
        count = lax.axis_size(axis)
        forward = [(i, i + 1) for i in range(count - 1)]
        forward.append((count - 1, 0))
        backward = [(target, source) for source, target in forward]
        low = lax.ppermute(
            lax.slice_in_dim(block, block.shape[dim] - width, None, axis=dim), axis, forward
        )
        high = lax.ppermute(lax.slice_in_dim(block, 0, width, axis=dim), axis, backward)
        block = jnp.concatenate([low, block, high], axis=dim)
    return block


def halo_parts(block):
    parts = []
    for axis, dim in (("circ", 1), ("span", 2)):
        count = lax.axis_size(axis)
        forward = [(i, (i + 1) % count) for i in range(count)]
        backward = [(target, source) for source, target in forward]
        low = lax.ppermute(lax.slice_in_dim(block, block.shape[dim] - 1, None, axis=dim), axis, forward)
        high = lax.ppermute(lax.slice_in_dim(block, 0, 1, axis=dim), axis, backward)
        parts += [low, high]
    span_index = lax.axis_index("span")
    span_last = lax.axis_size("span") - 1
    parts[2] = parts[2] * (span_index != 0).astype(block.dtype)
    parts[3] = parts[3] * (span_index != span_last).astype(block.dtype)
    return parts


def lateral_of(block, parts):
    circ_low, circ_high, span_low, span_high = parts
    return (
        jnp.concatenate([block[:, 1:], circ_high], axis=1),
        jnp.concatenate([circ_low, block[:, :-1]], axis=1),
        jnp.concatenate([block[:, :, 1:], span_high], axis=2),
        jnp.concatenate([span_low, block[:, :, :-1]], axis=2),
    )


def stencil_kernel(j_ref, c_ref, cu_ref, cd_ref, su_ref, sd_ref, prev_ref, rate_ref, out_ref):
    lane = lax.broadcasted_iota(jnp.int32, (8, 128), 1)
    probe = pltpu.roll(lane, 1, 1)
    numpy_order = probe == (lane + 127) % 128

    def chunk(i, carry):
        rows = pl.ds(pl.multiple_of(i * 8, 8), 8)
        cur = [c_ref[g, 0, rows, :] for g in range(NF)]
        cu = [cu_ref[g, 0, rows, :] for g in range(NF)]
        cd = [cd_ref[g, 0, rows, :] for g in range(NF)]
        su = [su_ref[g, 0, rows, :] for g in range(NF)]
        sd = [sd_ref[g, 0, rows, :] for g in range(NF)]
        au, ad = [], []
        for g in range(NF):
            one = pltpu.roll(cur[g], 1, 1)
            other = pltpu.roll(cur[g], 127, 1)
            down = jnp.where(numpy_order, one, other)
            up = jnp.where(numpy_order, other, one)
            ad.append(jnp.where(lane == 0, 0.0, down))
            au.append(jnp.where(lane == 127, 0.0, up))
        dc = [cu[g] - cd[g] for g in range(NF)]
        ds = [su[g] - sd[g] for g in range(NF)]
        da = [au[g] - ad[g] for g in range(NF)]
        rate = rate_ref[0, rows, :]
        for f in range(NF):
            convection = None
            for d, diff in enumerate((dc, ds, da)):
                term = j_ref[d * NF * NF + f * NF] * diff[0]
                for g in range(1, NF):
                    term = term + j_ref[d * NF * NF + f * NF + g] * diff[g]
                convection = term if convection is None else convection + term
            laplacian = cu[f] + cd[f] + (su[f] + sd[f]) + (au[f] + ad[f]) - 6.0 * cur[f]
            residual = (
                inv_step * (cur[f] - prev_ref[f, 0, rows, :])
                + 0.5 * convection
                - viscosity * laplacian
            )
            out_ref[f, 0, rows, :] = cur[f] - rate * residual
        return carry

    lax.fori_loop(0, c_ref.shape[2] // 8, chunk, 0)


def bulk_sweep(current, previous, rate_cells, jacobians):
    parts = halo_parts(current)
    circ_low, circ_high, span_low, span_high = parts
    padded = jnp.concatenate([circ_low, current, circ_high], axis=1)
    span_up = jnp.concatenate([current[:, :, 1:], span_high], axis=2)
    span_down = jnp.concatenate([span_low, current[:, :, :-1]], axis=2)
    nf, rows, span, axial = current.shape
    block = (nf, 1, span, axial)
    spec = lambda shift: pl.BlockSpec(block, lambda t: (0, t + shift, 0, 0))
    out = pl.pallas_call(
        stencil_kernel,
        grid=(rows,),
        in_specs=[
            pl.BlockSpec(memory_space=pltpu.SMEM),
            spec(1),
            spec(2),
            spec(0),
            spec(0),
            spec(0),
            spec(0),
            pl.BlockSpec((1, span, axial), lambda t: (t, 0, 0)),
        ],
        out_specs=spec(0),
        out_shape=jax.ShapeDtypeStruct(current.shape, current.dtype),
    )(jacobians.reshape(-1), padded, padded, padded, span_up, span_down, previous, rate_cells)
    return out, parts


def contract(matrix, values):
    column = lambda g: matrix[:, g].reshape((-1,) + (1,) * (values.ndim - 1))
    total = column(0) * values[0][None]
    for g in range(1, matrix.shape[1]):
        total = total + column(g) * values[g][None]
    return total


def update(current, previous, rate_cells, neighbours, jacobians):
    circ_up, circ_down, span_up, span_down, axial_up, axial_down = neighbours
    convection = contract(jacobians[0], circ_up - circ_down)
    convection = convection + contract(jacobians[1], span_up - span_down)
    convection = convection + contract(jacobians[2], axial_up - axial_down)
    laplacian = (
        circ_up + circ_down + (span_up + span_down) + (axial_up + axial_down) - 6.0 * current
    )
    residual = inv_step * (current - previous) + 0.5 * convection - viscosity * laplacian
    return current - rate_cells[None] * residual


def lateral(padded):
    return (
        padded[:, 2:, 1:-1],
        padded[:, :-2, 1:-1],
        padded[:, 1:-1, 2:],
        padded[:, 1:-1, :-2],
    )


def advance(padded, current, previous, rate_cells, jacobians):
    zero_column = jnp.zeros_like(current[..., :1])
    axial_up = jnp.concatenate([current[..., 1:], zero_column], axis=-1)
    axial_down = jnp.concatenate([zero_column, current[..., :-1]], axis=-1)
    neighbours = lateral(padded) + (axial_up, axial_down)
    return update(current, previous, rate_cells, neighbours, jacobians)


def wall_zero(field_array, width):
    span_index = lax.axis_index("span")
    span_count = lax.axis_size("span")
    length = field_array.shape[2]
    position = jnp.arange(length, dtype=jnp.int32)
    at_hub = jnp.logical_and(span_index == 0, position < width)
    at_tip = jnp.logical_and(span_index == span_count - 1, position >= length - width)
    keeping = jnp.logical_not(jnp.logical_or(at_hub, at_tip)).astype(field_array.dtype)
    keeping = keeping.reshape(1, 1, length, 1)
    return field_array * keeping


def body(
    q_old, pseudo_rate, flux_jacobians, rotor_face, offsets, owners, slots, weight_idx, weight_table
):
    circ_count = lax.axis_size("circ")
    span_count = lax.axis_size("span")
    rows_local = rotor_face.shape[1]
    total_rows = rows_local * circ_count
    copies = jnp.broadcast_to(rotor_face[None], (circ_count,) + rotor_face.shape)
    gathered = lax.all_to_all(copies, "circ", 0, 0, tiled=True)
    row_iota = jnp.arange(rows_local, dtype=jnp.int32)
    first_row = lax.axis_index("circ") * rows_local
    source_rows = (first_row + row_iota[:, None] - offsets[None, :]) % total_rows
    global_rows = jnp.arange(total_rows, dtype=jnp.int32).reshape(circ_count, rows_local)
    picks = global_rows[:, None, :, None, None] == source_rows[None, None, None]
    rotated = jnp.sum(
        jnp.where(picks, gathered[:, :, :, None, :], 0.0), axis=(0, 2)
    )
    panels = rotated.reshape(NF, rows_local, KP_DEV, PW)
    table_ids = jnp.arange(weight_table.shape[0], dtype=jnp.int32)
    weights = jnp.sum(jnp.where(weight_idx[..., None] == table_ids, weight_table, 0.0), axis=-1)
    targets = owners[0] * KP_DEV + slots[0]
    local_weights = weights[0]
    panel_ids = jnp.arange(KP_DEV * span_count, dtype=jnp.int32)
    mixing = jnp.sum(
        jnp.where(targets[None] == panel_ids[:, None, None], local_weights[None], 0.0), axis=-1
    ).reshape(span_count, KP_DEV, KP_DEV)
    contributions = jnp.einsum(
        "ogk,ftkp->oftgp", mixing, panels, precision=lax.Precision.HIGHEST
    ).reshape(span_count, NF, rows_local, KP_DEV * PW)
    received = lax.all_to_all(contributions, "span", 0, 0, tiled=True)
    inlet_plane = jnp.sum(received, axis=0)

    mid_bulk, old_parts = bulk_sweep(q_old, q_old, pseudo_rate, flux_jacobians)
    new_bulk, mid_parts = bulk_sweep(mid_bulk, q_old, pseudo_rate, flux_jacobians)

    old_first, old_second = q_old[..., 0], q_old[..., 1]
    rate_first, rate_second = pseudo_rate[..., 0], pseudo_rate[..., 1]
    mid_second, mid_third = mid_bulk[..., 1], mid_bulk[..., 2]
    old_lateral = lateral_of(old_first, [p[..., 0] for p in old_parts])
    mid_first = update(
        old_first, old_first, rate_first, old_lateral + (old_second, inlet_plane), flux_jacobians
    )
    first_lateral = lateral_of(mid_first, halo_parts(mid_first))
    new_first = update(
        mid_first, old_first, rate_first, first_lateral + (mid_second, inlet_plane), flux_jacobians
    )
    second_lateral = lateral_of(mid_second, [p[..., 1] for p in mid_parts])
    new_second = update(
        mid_second, old_second, rate_second, second_lateral + (mid_third, mid_first), flux_jacobians
    )
    return new_bulk.at[..., 0].set(new_first).at[..., 1].set(new_second)


def solution(mesh):
    return jax.shard_map(
        body,
        mesh=mesh,
        in_specs=(
            P(None, "circ", "span", None),
            P("circ", "span", None),
            P(),
            P(None, "circ", "span"),
            P("span"),
            P("circ", "span", None),
            P("circ", "span", None),
            P("circ", "span", None),
            P(),
        ),
        out_specs=P(None, "circ", "span", None),
        check_vma=False,
    )
```

```python
import jax
import jax.numpy as jnp
from jax import lax
from jax.experimental import pallas as pl
from jax.experimental.pallas import tpu as pltpu
from jax.sharding import PartitionSpec as P

NF = 5
KP_DEV = 4
PW = 32


inv_step = 0.5
viscosity = 0.1


def with_halo(block, sides, width):
    for axis, dim in sides:
        count = lax.axis_size(axis)
        forward = [(i, i + 1) for i in range(count - 1)]
        forward.append((count - 1, 0))
        backward = [(target, source) for source, target in forward]
        low = lax.ppermute(
            lax.slice_in_dim(block, block.shape[dim] - width, None, axis=dim), axis, forward
        )
        high = lax.ppermute(lax.slice_in_dim(block, 0, width, axis=dim), axis, backward)
        block = jnp.concatenate([low, block, high], axis=dim)
    return block


def halo_parts(block):
    parts = []
    for axis, dim in (("circ", 1), ("span", 2)):
        count = lax.axis_size(axis)
        forward = [(i, (i + 1) % count) for i in range(count)]
        backward = [(target, source) for source, target in forward]
        low = lax.ppermute(lax.slice_in_dim(block, block.shape[dim] - 1, None, axis=dim), axis, forward)
        high = lax.ppermute(lax.slice_in_dim(block, 0, 1, axis=dim), axis, backward)
        parts += [low, high]
    span_index = lax.axis_index("span")
    span_last = lax.axis_size("span") - 1
    parts[2] = parts[2] * (span_index != 0).astype(block.dtype)
    parts[3] = parts[3] * (span_index != span_last).astype(block.dtype)
    return parts


def lateral_of(block, parts):
    circ_low, circ_high, span_low, span_high = parts
    return (
        jnp.concatenate([block[:, 1:], circ_high], axis=1),
        jnp.concatenate([circ_low, block[:, :-1]], axis=1),
        jnp.concatenate([block[:, :, 1:], span_high], axis=2),
        jnp.concatenate([span_low, block[:, :, :-1]], axis=2),
    )


def stencil_kernel(j_ref, c_ref, cu_ref, cd_ref, su_ref, sd_ref, prev_ref, rate_ref, inlet_ref, out_ref):
    lane = lax.broadcasted_iota(jnp.int32, (8, 128), 1)
    probe = pltpu.roll(lane, 1, 1)
    numpy_order = probe == (lane + 127) % 128

    def chunk(i, carry):
        rows = pl.ds(pl.multiple_of(i * 8, 8), 8)
        cur = [c_ref[g, 0, rows, :] for g in range(NF)]
        cu = [cu_ref[g, 0, rows, :] for g in range(NF)]
        cd = [cd_ref[g, 0, rows, :] for g in range(NF)]
        su = [su_ref[g, 0, rows, :] for g in range(NF)]
        sd = [sd_ref[g, 0, rows, :] for g in range(NF)]
        au, ad = [], []
        for g in range(NF):
            one = pltpu.roll(cur[g], 1, 1)
            other = pltpu.roll(cur[g], 127, 1)
            down = jnp.where(numpy_order, one, other)
            up = jnp.where(numpy_order, other, one)
            ad.append(jnp.where(lane == 0, inlet_ref[g, 0, rows, :], down))
            au.append(jnp.where(lane == 127, 0.0, up))
        dc = [cu[g] - cd[g] for g in range(NF)]
        ds = [su[g] - sd[g] for g in range(NF)]
        da = [au[g] - ad[g] for g in range(NF)]
        rate = rate_ref[0, rows, :]
        for f in range(NF):
            convection = None
            for d, diff in enumerate((dc, ds, da)):
                term = j_ref[d * NF * NF + f * NF] * diff[0]
                for g in range(1, NF):
                    term = term + j_ref[d * NF * NF + f * NF + g] * diff[g]
                convection = term if convection is None else convection + term
            laplacian = cu[f] + cd[f] + (su[f] + sd[f]) + (au[f] + ad[f]) - 6.0 * cur[f]
            residual = (
                inv_step * (cur[f] - prev_ref[f, 0, rows, :])
                + 0.5 * convection
                - viscosity * laplacian
            )
            out_ref[f, 0, rows, :] = cur[f] - rate * residual
        return carry

    lax.fori_loop(0, c_ref.shape[2] // 8, chunk, 0)


def sweep(current, previous, rate_cells, inlet_column, jacobians):
    parts = halo_parts(current)
    circ_low, circ_high, span_low, span_high = parts
    padded = jnp.concatenate([circ_low, current, circ_high], axis=1)
    span_up = jnp.concatenate([current[:, :, 1:], span_high], axis=2)
    span_down = jnp.concatenate([span_low, current[:, :, :-1]], axis=2)
    nf, rows, span, axial = current.shape
    block = (nf, 1, span, axial)
    spec = lambda shift: pl.BlockSpec(block, lambda t: (0, t + shift, 0, 0))
    out = pl.pallas_call(
        stencil_kernel,
        grid=(rows,),
        in_specs=[
            pl.BlockSpec(memory_space=pltpu.SMEM),
            spec(1),
            spec(2),
            spec(0),
            spec(0),
            spec(0),
            spec(0),
            pl.BlockSpec((1, span, axial), lambda t: (t, 0, 0)),
            pl.BlockSpec((nf, 1, span, 1), lambda t: (0, t, 0, 0)),
        ],
        out_specs=spec(0),
        out_shape=jax.ShapeDtypeStruct(current.shape, current.dtype),
    )(jacobians.reshape(-1), padded, padded, padded, span_up, span_down, previous, rate_cells, inlet_column)
    return out, parts


def contract(matrix, values):
    column = lambda g: matrix[:, g].reshape((-1,) + (1,) * (values.ndim - 1))
    total = column(0) * values[0][None]
    for g in range(1, matrix.shape[1]):
        total = total + column(g) * values[g][None]
    return total


def update(current, previous, rate_cells, neighbours, jacobians):
    circ_up, circ_down, span_up, span_down, axial_up, axial_down = neighbours
    convection = contract(jacobians[0], circ_up - circ_down)
    convection = convection + contract(jacobians[1], span_up - span_down)
    convection = convection + contract(jacobians[2], axial_up - axial_down)
    laplacian = (
        circ_up + circ_down + (span_up + span_down) + (axial_up + axial_down) - 6.0 * current
    )
    residual = inv_step * (current - previous) + 0.5 * convection - viscosity * laplacian
    return current - rate_cells[None] * residual


def lateral(padded):
    return (
        padded[:, 2:, 1:-1],
        padded[:, :-2, 1:-1],
        padded[:, 1:-1, 2:],
        padded[:, 1:-1, :-2],
    )


def advance(padded, current, previous, rate_cells, jacobians):
    zero_column = jnp.zeros_like(current[..., :1])
    axial_up = jnp.concatenate([current[..., 1:], zero_column], axis=-1)
    axial_down = jnp.concatenate([zero_column, current[..., :-1]], axis=-1)
    neighbours = lateral(padded) + (axial_up, axial_down)
    return update(current, previous, rate_cells, neighbours, jacobians)


def wall_zero(field_array, width):
    span_index = lax.axis_index("span")
    span_count = lax.axis_size("span")
    length = field_array.shape[2]
    position = jnp.arange(length, dtype=jnp.int32)
    at_hub = jnp.logical_and(span_index == 0, position < width)
    at_tip = jnp.logical_and(span_index == span_count - 1, position >= length - width)
    keeping = jnp.logical_not(jnp.logical_or(at_hub, at_tip)).astype(field_array.dtype)
    keeping = keeping.reshape(1, 1, length, 1)
    return field_array * keeping


def body(
    q_old, pseudo_rate, flux_jacobians, rotor_face, offsets, owners, slots, weight_idx, weight_table
):
    circ_count = lax.axis_size("circ")
    span_count = lax.axis_size("span")
    rows_local = rotor_face.shape[1]
    total_rows = rows_local * circ_count
    copies = jnp.broadcast_to(rotor_face[None], (circ_count,) + rotor_face.shape)
    gathered = lax.all_to_all(copies, "circ", 0, 0, tiled=True)
    row_iota = jnp.arange(rows_local, dtype=jnp.int32)
    first_row = lax.axis_index("circ") * rows_local
    source_rows = (first_row + row_iota[:, None] - offsets[None, :]) % total_rows
    global_rows = jnp.arange(total_rows, dtype=jnp.int32).reshape(circ_count, rows_local)
    picks = global_rows[:, None, :, None, None] == source_rows[None, None, None]
    rotated = jnp.sum(
        jnp.where(picks, gathered[:, :, :, None, :], 0.0), axis=(0, 2)
    )
    panels = rotated.reshape(NF, rows_local, KP_DEV, PW)
    table_ids = jnp.arange(weight_table.shape[0], dtype=jnp.int32)
    weights = jnp.sum(jnp.where(weight_idx[..., None] == table_ids, weight_table, 0.0), axis=-1)
    targets = owners[0] * KP_DEV + slots[0]
    local_weights = weights[0]
    panel_ids = jnp.arange(KP_DEV * span_count, dtype=jnp.int32)
    mixing = jnp.sum(
        jnp.where(targets[None] == panel_ids[:, None, None], local_weights[None], 0.0), axis=-1
    ).reshape(span_count, KP_DEV, KP_DEV)
    contributions = jnp.einsum(
        "ogk,ftkp->oftgp", mixing, panels, precision=lax.Precision.HIGHEST
    ).reshape(span_count, NF, rows_local, KP_DEV * PW)
    received = lax.all_to_all(contributions, "span", 0, 0, tiled=True)
    inlet_plane = jnp.sum(received, axis=0)

    inlet_column = inlet_plane[..., None]
    mid, _ = sweep(q_old, q_old, pseudo_rate, inlet_column, flux_jacobians)
    new, _ = sweep(mid, q_old, pseudo_rate, inlet_column, flux_jacobians)
    return new


def solution(mesh):
    return jax.shard_map(
        body,
        mesh=mesh,
        in_specs=(
            P(None, "circ", "span", None),
            P("circ", "span", None),
            P(),
            P(None, "circ", "span"),
            P("span"),
            P("circ", "span", None),
            P("circ", "span", None),
            P("circ", "span", None),
            P(),
        ),
        out_specs=P(None, "circ", "span", None),
        check_vma=False,
    )
```

```python
import jax
import jax.numpy as jnp
from jax import lax
from jax.experimental import pallas as pl
from jax.experimental.pallas import tpu as pltpu
from jax.sharding import PartitionSpec as P

NF = 5
KP_DEV = 4
PW = 32


inv_step = 0.5
viscosity = 0.1


def with_halo(block, sides, width):
    for axis, dim in sides:
        count = lax.axis_size(axis)
        forward = [(i, i + 1) for i in range(count - 1)]
        forward.append((count - 1, 0))
        backward = [(target, source) for source, target in forward]
        low = lax.ppermute(
            lax.slice_in_dim(block, block.shape[dim] - width, None, axis=dim), axis, forward
        )
        high = lax.ppermute(lax.slice_in_dim(block, 0, width, axis=dim), axis, backward)
        block = jnp.concatenate([low, block, high], axis=dim)
    return block


def halo_parts(block):
    parts = []
    for axis, dim in (("circ", 1), ("span", 2)):
        count = lax.axis_size(axis)
        forward = [(i, (i + 1) % count) for i in range(count)]
        backward = [(target, source) for source, target in forward]
        low = lax.ppermute(lax.slice_in_dim(block, block.shape[dim] - 1, None, axis=dim), axis, forward)
        high = lax.ppermute(lax.slice_in_dim(block, 0, 1, axis=dim), axis, backward)
        parts += [low, high]
    span_index = lax.axis_index("span")
    span_last = lax.axis_size("span") - 1
    parts[2] = parts[2] * (span_index != 0).astype(block.dtype)
    parts[3] = parts[3] * (span_index != span_last).astype(block.dtype)
    return parts


def lateral_of(block, parts):
    circ_low, circ_high, span_low, span_high = parts
    return (
        jnp.concatenate([block[:, 1:], circ_high], axis=1),
        jnp.concatenate([circ_low, block[:, :-1]], axis=1),
        jnp.concatenate([block[:, :, 1:], span_high], axis=2),
        jnp.concatenate([span_low, block[:, :, :-1]], axis=2),
    )


def stencil_kernel(j_ref, c_ref, cu_ref, cd_ref, su_ref, sd_ref, prev_ref, rate_ref, inlet_ref, out_ref):
    lane = lax.broadcasted_iota(jnp.int32, (8, 128), 1)
    probe = pltpu.roll(lane, 1, 1)
    numpy_order = probe == (lane + 127) % 128

    def chunk(i, carry):
        rows = pl.ds(pl.multiple_of(i * 8, 8), 8)
        cur = [c_ref[g, 0, rows, :] for g in range(NF)]
        cu = [cu_ref[g, 0, rows, :] for g in range(NF)]
        cd = [cd_ref[g, 0, rows, :] for g in range(NF)]
        su = [su_ref[g, 0, rows, :] for g in range(NF)]
        sd = [sd_ref[g, 0, rows, :] for g in range(NF)]
        au, ad = [], []
        for g in range(NF):
            one = pltpu.roll(cur[g], 1, 1)
            other = pltpu.roll(cur[g], 127, 1)
            down = jnp.where(numpy_order, one, other)
            up = jnp.where(numpy_order, other, one)
            ad.append(jnp.where(lane == 0, inlet_ref[g, 0, rows, :], down))
            au.append(jnp.where(lane == 127, 0.0, up))
        dc = [cu[g] - cd[g] for g in range(NF)]
        ds = [su[g] - sd[g] for g in range(NF)]
        da = [au[g] - ad[g] for g in range(NF)]
        rate = rate_ref[0, rows, :]
        for f in range(NF):
            convection = None
            for d, diff in enumerate((dc, ds, da)):
                term = j_ref[d * NF * NF + f * NF] * diff[0]
                for g in range(1, NF):
                    term = term + j_ref[d * NF * NF + f * NF + g] * diff[g]
                convection = term if convection is None else convection + term
            laplacian = cu[f] + cd[f] + (su[f] + sd[f]) + (au[f] + ad[f]) - 6.0 * cur[f]
            residual = (
                inv_step * (cur[f] - prev_ref[f, 0, rows, :])
                + 0.5 * convection
                - viscosity * laplacian
            )
            out_ref[f, 0, rows, :] = cur[f] - rate * residual
        return carry

    lax.fori_loop(0, c_ref.shape[2] // 8, chunk, 0)


def sweep(current, previous, rate_cells, inlet_column, jacobians, parts=None):
    if parts is None:
        parts = halo_parts(current)
    circ_low, circ_high, span_low, span_high = parts
    padded = jnp.concatenate([circ_low, current, circ_high], axis=1)
    span_up = jnp.concatenate([current[:, :, 1:], span_high], axis=2)
    span_down = jnp.concatenate([span_low, current[:, :, :-1]], axis=2)
    nf, rows, span, axial = current.shape
    block = (nf, 1, span, axial)
    spec = lambda shift: pl.BlockSpec(block, lambda t: (0, t + shift, 0, 0))
    out = pl.pallas_call(
        stencil_kernel,
        grid=(rows,),
        in_specs=[
            pl.BlockSpec(memory_space=pltpu.SMEM),
            spec(1),
            spec(2),
            spec(0),
            spec(0),
            spec(0),
            spec(0),
            pl.BlockSpec((1, span, axial), lambda t: (t, 0, 0)),
            pl.BlockSpec((nf, 1, span, 1), lambda t: (0, t, 0, 0)),
        ],
        out_specs=spec(0),
        out_shape=jax.ShapeDtypeStruct(current.shape, current.dtype),
    )(jacobians.reshape(-1), padded, padded, padded, span_up, span_down, previous, rate_cells, inlet_column)
    return out, parts


def contract(matrix, values):
    column = lambda g: matrix[:, g].reshape((-1,) + (1,) * (values.ndim - 1))
    total = column(0) * values[0][None]
    for g in range(1, matrix.shape[1]):
        total = total + column(g) * values[g][None]
    return total


def update(current, previous, rate_cells, neighbours, jacobians):
    circ_up, circ_down, span_up, span_down, axial_up, axial_down = neighbours
    convection = contract(jacobians[0], circ_up - circ_down)
    convection = convection + contract(jacobians[1], span_up - span_down)
    convection = convection + contract(jacobians[2], axial_up - axial_down)
    laplacian = (
        circ_up + circ_down + (span_up + span_down) + (axial_up + axial_down) - 6.0 * current
    )
    residual = inv_step * (current - previous) + 0.5 * convection - viscosity * laplacian
    return current - rate_cells[None] * residual


def lateral(padded):
    return (
        padded[:, 2:, 1:-1],
        padded[:, :-2, 1:-1],
        padded[:, 1:-1, 2:],
        padded[:, 1:-1, :-2],
    )


def advance(padded, current, previous, rate_cells, jacobians):
    zero_column = jnp.zeros_like(current[..., :1])
    axial_up = jnp.concatenate([current[..., 1:], zero_column], axis=-1)
    axial_down = jnp.concatenate([zero_column, current[..., :-1]], axis=-1)
    neighbours = lateral(padded) + (axial_up, axial_down)
    return update(current, previous, rate_cells, neighbours, jacobians)


def wall_zero(field_array, width):
    span_index = lax.axis_index("span")
    span_count = lax.axis_size("span")
    length = field_array.shape[2]
    position = jnp.arange(length, dtype=jnp.int32)
    at_hub = jnp.logical_and(span_index == 0, position < width)
    at_tip = jnp.logical_and(span_index == span_count - 1, position >= length - width)
    keeping = jnp.logical_not(jnp.logical_or(at_hub, at_tip)).astype(field_array.dtype)
    keeping = keeping.reshape(1, 1, length, 1)
    return field_array * keeping


def body(
    q_old, pseudo_rate, flux_jacobians, rotor_face, offsets, owners, slots, weight_idx, weight_table
):
    circ_count = lax.axis_size("circ")
    span_count = lax.axis_size("span")
    rows_local = rotor_face.shape[1]
    total_rows = rows_local * circ_count
    copies = jnp.broadcast_to(rotor_face[None], (circ_count,) + rotor_face.shape)
    gathered = lax.all_to_all(copies, "circ", 0, 0, tiled=True)
    row_iota = jnp.arange(rows_local, dtype=jnp.int32)
    first_row = lax.axis_index("circ") * rows_local
    source_rows = (first_row + row_iota[:, None] - offsets[None, :]) % total_rows
    global_rows = jnp.arange(total_rows, dtype=jnp.int32).reshape(circ_count, rows_local)
    picks = global_rows[:, None, :, None, None] == source_rows[None, None, None]
    rotated = jnp.sum(
        jnp.where(picks, gathered[:, :, :, None, :], 0.0), axis=(0, 2)
    )
    panels = rotated.reshape(NF, rows_local, KP_DEV, PW)
    table_ids = jnp.arange(weight_table.shape[0], dtype=jnp.int32)
    weights = jnp.sum(jnp.where(weight_idx[..., None] == table_ids, weight_table, 0.0), axis=-1)
    targets = owners[0] * KP_DEV + slots[0]
    local_weights = weights[0]
    panel_ids = jnp.arange(KP_DEV * span_count, dtype=jnp.int32)
    mixing = jnp.sum(
        jnp.where(targets[None] == panel_ids[:, None, None], local_weights[None], 0.0), axis=-1
    ).reshape(span_count, KP_DEV, KP_DEV)
    contributions = jnp.einsum(
        "ogk,ftkp->oftgp", mixing, panels, precision=lax.Precision.HIGHEST
    ).reshape(span_count, NF, rows_local, KP_DEV * PW)
    received = lax.all_to_all(contributions, "span", 0, 0, tiled=True)
    inlet_plane = jnp.sum(received, axis=0)

    inlet_column = inlet_plane[..., None]
    mid_bulk, _ = sweep(q_old, q_old, pseudo_rate, jnp.zeros_like(inlet_column), flux_jacobians)
    bulk_parts = halo_parts(mid_bulk)
    correction = pseudo_rate[None, :, :, :1] * (
        0.5 * contract(flux_jacobians[2], inlet_column) + viscosity * inlet_column
    )
    at_inlet = lax.broadcasted_iota(jnp.int32, q_old.shape, 3) == 0
    mid = jnp.where(at_inlet, mid_bulk + correction, mid_bulk)
    mid_parts = [
        jnp.where(lax.broadcasted_iota(jnp.int32, bulk.shape, 3) == 0, bulk + extra, bulk)
        for bulk, extra in zip(bulk_parts, halo_parts(correction))
    ]
    new, _ = sweep(mid, q_old, pseudo_rate, inlet_column, flux_jacobians, mid_parts)
    return new


def solution(mesh):
    return jax.shard_map(
        body,
        mesh=mesh,
        in_specs=(
            P(None, "circ", "span", None),
            P("circ", "span", None),
            P(),
            P(None, "circ", "span"),
            P("span"),
            P("circ", "span", None),
            P("circ", "span", None),
            P("circ", "span", None),
            P(),
        ),
        out_specs=P(None, "circ", "span", None),
        check_vma=False,
    )
```

```python
import jax
import jax.numpy as jnp
from jax import lax
from jax.experimental import pallas as pl
from jax.experimental.pallas import tpu as pltpu
from jax.sharding import PartitionSpec as P

NF = 5
KP_DEV = 4
PW = 32


inv_step = 0.5
viscosity = 0.1


def with_halo(block, sides, width):
    for axis, dim in sides:
        count = lax.axis_size(axis)
        forward = [(i, i + 1) for i in range(count - 1)]
        forward.append((count - 1, 0))
        backward = [(target, source) for source, target in forward]
        low = lax.ppermute(
            lax.slice_in_dim(block, block.shape[dim] - width, None, axis=dim), axis, forward
        )
        high = lax.ppermute(lax.slice_in_dim(block, 0, width, axis=dim), axis, backward)
        block = jnp.concatenate([low, block, high], axis=dim)
    return block


def halo_parts(block):
    parts = []
    for axis, dim in (("circ", 1), ("span", 2)):
        count = lax.axis_size(axis)
        forward = [(i, (i + 1) % count) for i in range(count)]
        backward = [(target, source) for source, target in forward]
        low = lax.ppermute(lax.slice_in_dim(block, block.shape[dim] - 1, None, axis=dim), axis, forward)
        high = lax.ppermute(lax.slice_in_dim(block, 0, 1, axis=dim), axis, backward)
        parts += [low, high]
    span_index = lax.axis_index("span")
    span_last = lax.axis_size("span") - 1
    parts[2] = parts[2] * (span_index != 0).astype(block.dtype)
    parts[3] = parts[3] * (span_index != span_last).astype(block.dtype)
    return parts


def lateral_of(block, parts):
    circ_low, circ_high, span_low, span_high = parts
    return (
        jnp.concatenate([block[:, 1:], circ_high], axis=1),
        jnp.concatenate([circ_low, block[:, :-1]], axis=1),
        jnp.concatenate([block[:, :, 1:], span_high], axis=2),
        jnp.concatenate([span_low, block[:, :, :-1]], axis=2),
    )


def stencil_kernel(j_ref, c_ref, cu_ref, cd_ref, su_ref, sd_ref, prev_ref, rate_ref, inlet_ref, out_ref):
    lane = lax.broadcasted_iota(jnp.int32, (8, 128), 1)
    probe = pltpu.roll(lane, 1, 1)
    numpy_order = probe == (lane + 127) % 128

    def chunk(i, carry):
        rows = pl.ds(pl.multiple_of(i * 8, 8), 8)
        cur = [c_ref[g, 0, rows, :] for g in range(NF)]
        cu = [cu_ref[g, 0, rows, :] for g in range(NF)]
        cd = [cd_ref[g, 0, rows, :] for g in range(NF)]
        su = [su_ref[g, 0, rows, :] for g in range(NF)]
        sd = [sd_ref[g, 0, rows, :] for g in range(NF)]
        au, ad = [], []
        for g in range(NF):
            one = pltpu.roll(cur[g], 1, 1)
            other = pltpu.roll(cur[g], 127, 1)
            down = jnp.where(numpy_order, one, other)
            up = jnp.where(numpy_order, other, one)
            ad.append(jnp.where(lane == 0, inlet_ref[g, 0, rows, :], down))
            au.append(jnp.where(lane == 127, 0.0, up))
        dc = [cu[g] - cd[g] for g in range(NF)]
        ds = [su[g] - sd[g] for g in range(NF)]
        da = [au[g] - ad[g] for g in range(NF)]
        rate = rate_ref[0, rows, :]
        for f in range(NF):
            convection = None
            for d, diff in enumerate((dc, ds, da)):
                term = j_ref[d * NF * NF + f * NF] * diff[0]
                for g in range(1, NF):
                    term = term + j_ref[d * NF * NF + f * NF + g] * diff[g]
                convection = term if convection is None else convection + term
            laplacian = cu[f] + cd[f] + (su[f] + sd[f]) + (au[f] + ad[f]) - 6.0 * cur[f]
            residual = (
                inv_step * (cur[f] - prev_ref[f, 0, rows, :])
                + 0.5 * convection
                - viscosity * laplacian
            )
            out_ref[f, 0, rows, :] = cur[f] - rate * residual
        return carry

    lax.fori_loop(0, c_ref.shape[2] // 8, chunk, 0)


def sweep(current, previous, rate_cells, inlet_column, jacobians, parts=None):
    if parts is None:
        parts = halo_parts(current)
    circ_low, circ_high, span_low, span_high = parts
    padded = jnp.concatenate([circ_low, current, circ_high], axis=1)
    span_up = jnp.concatenate([current[:, :, 1:], span_high], axis=2)
    span_down = jnp.concatenate([span_low, current[:, :, :-1]], axis=2)
    nf, rows, span, axial = current.shape
    block = (nf, 1, span, axial)
    spec = lambda shift: pl.BlockSpec(block, lambda t: (0, t + shift, 0, 0))
    out = pl.pallas_call(
        stencil_kernel,
        grid=(rows,),
        in_specs=[
            pl.BlockSpec(memory_space=pltpu.SMEM),
            spec(1),
            spec(2),
            spec(0),
            spec(0),
            spec(0),
            spec(0),
            pl.BlockSpec((1, span, axial), lambda t: (t, 0, 0)),
            pl.BlockSpec((nf, 1, span, 1), lambda t: (0, t, 0, 0)),
        ],
        out_specs=spec(0),
        out_shape=jax.ShapeDtypeStruct(current.shape, current.dtype),
    )(jacobians.reshape(-1), padded, padded, padded, span_up, span_down, previous, rate_cells, inlet_column)
    return out, parts


def contract(matrix, values):
    column = lambda g: matrix[:, g].reshape((-1,) + (1,) * (values.ndim - 1))
    total = column(0) * values[0][None]
    for g in range(1, matrix.shape[1]):
        total = total + column(g) * values[g][None]
    return total


def update(current, previous, rate_cells, neighbours, jacobians):
    circ_up, circ_down, span_up, span_down, axial_up, axial_down = neighbours
    convection = contract(jacobians[0], circ_up - circ_down)
    convection = convection + contract(jacobians[1], span_up - span_down)
    convection = convection + contract(jacobians[2], axial_up - axial_down)
    laplacian = (
        circ_up + circ_down + (span_up + span_down) + (axial_up + axial_down) - 6.0 * current
    )
    residual = inv_step * (current - previous) + 0.5 * convection - viscosity * laplacian
    return current - rate_cells[None] * residual


def lateral(padded):
    return (
        padded[:, 2:, 1:-1],
        padded[:, :-2, 1:-1],
        padded[:, 1:-1, 2:],
        padded[:, 1:-1, :-2],
    )


def advance(padded, current, previous, rate_cells, jacobians):
    zero_column = jnp.zeros_like(current[..., :1])
    axial_up = jnp.concatenate([current[..., 1:], zero_column], axis=-1)
    axial_down = jnp.concatenate([zero_column, current[..., :-1]], axis=-1)
    neighbours = lateral(padded) + (axial_up, axial_down)
    return update(current, previous, rate_cells, neighbours, jacobians)


def wall_zero(field_array, width):
    span_index = lax.axis_index("span")
    span_count = lax.axis_size("span")
    length = field_array.shape[2]
    position = jnp.arange(length, dtype=jnp.int32)
    at_hub = jnp.logical_and(span_index == 0, position < width)
    at_tip = jnp.logical_and(span_index == span_count - 1, position >= length - width)
    keeping = jnp.logical_not(jnp.logical_or(at_hub, at_tip)).astype(field_array.dtype)
    keeping = keeping.reshape(1, 1, length, 1)
    return field_array * keeping


def body(
    q_old, pseudo_rate, flux_jacobians, rotor_face, offsets, owners, slots, weight_idx, weight_table
):
    circ_count = lax.axis_size("circ")
    span_count = lax.axis_size("span")
    rows_local = rotor_face.shape[1]
    total_rows = rows_local * circ_count
    copies = jnp.broadcast_to(rotor_face[None], (circ_count,) + rotor_face.shape)
    gathered = lax.all_to_all(copies, "circ", 0, 0, tiled=True)
    row_iota = jnp.arange(rows_local, dtype=jnp.int32)
    first_row = lax.axis_index("circ") * rows_local
    source_rows = (first_row + row_iota[:, None] - offsets[None, :]) % total_rows
    global_rows = jnp.arange(total_rows, dtype=jnp.int32).reshape(circ_count, rows_local)
    picks = global_rows[:, None, :, None, None] == source_rows[None, None, None]
    rotated = jnp.sum(
        jnp.where(picks, gathered[:, :, :, None, :], 0.0), axis=(0, 2)
    )
    panels = rotated.reshape(NF, rows_local, KP_DEV, PW)
    table_ids = jnp.arange(weight_table.shape[0], dtype=jnp.int32)
    weights = jnp.sum(jnp.where(weight_idx[..., None] == table_ids, weight_table, 0.0), axis=-1)
    targets = owners[0] * KP_DEV + slots[0]
    local_weights = weights[0]
    panel_ids = jnp.arange(KP_DEV * span_count, dtype=jnp.int32)
    mixing = jnp.sum(
        jnp.where(targets[None] == panel_ids[:, None, None], local_weights[None], 0.0), axis=-1
    ).reshape(span_count, KP_DEV, KP_DEV)
    contributions = jnp.einsum(
        "ogk,ftkp->oftgp", mixing, panels, precision=lax.Precision.HIGHEST
    ).reshape(span_count, NF, rows_local, KP_DEV * PW)
    received = lax.all_to_all(contributions, "span", 0, 0, tiled=True)
    inlet_plane = jnp.sum(received, axis=0)

    inlet_column = inlet_plane[..., None]
    contributions, q_for_halo = lax.optimization_barrier((contributions, q_old))
    mid, _ = sweep(q_old, q_old, pseudo_rate, inlet_column, flux_jacobians, halo_parts(q_for_halo))
    mid_parts = halo_parts(mid)
    zero_parts = [jnp.zeros_like(p) for p in mid_parts]
    new, _ = sweep(mid, q_old, pseudo_rate, inlet_column, flux_jacobians, zero_parts)
    circ_low, circ_high, span_low, span_high = mid_parts
    eye = jnp.eye(NF, dtype=q_old.dtype)
    from_low = lambda d: 0.5 * flux_jacobians[d] + viscosity * eye
    from_high = lambda d: viscosity * eye - 0.5 * flux_jacobians[d]
    rate = pseudo_rate[None]
    new = new.at[:, :1].add(rate[:, :1] * contract(from_low(0), circ_low))
    new = new.at[:, -1:].add(rate[:, -1:] * contract(from_high(0), circ_high))
    new = new.at[:, :, :1].add(rate[:, :, :1] * contract(from_low(1), span_low))
    new = new.at[:, :, -1:].add(rate[:, :, -1:] * contract(from_high(1), span_high))
    return new


def solution(mesh):
    return jax.shard_map(
        body,
        mesh=mesh,
        in_specs=(
            P(None, "circ", "span", None),
            P("circ", "span", None),
            P(),
            P(None, "circ", "span"),
            P("span"),
            P("circ", "span", None),
            P("circ", "span", None),
            P("circ", "span", None),
            P(),
        ),
        out_specs=P(None, "circ", "span", None),
        check_vma=False,
    )
```

```python
import jax
import jax.numpy as jnp
from jax import lax
from jax.experimental import pallas as pl
from jax.experimental.pallas import tpu as pltpu
from jax.sharding import PartitionSpec as P

NF = 5
KP_DEV = 4
PW = 32


inv_step = 0.5
viscosity = 0.1


def halo_parts(block):
    parts = []
    for axis, dim in (("circ", 1), ("span", 2)):
        count = lax.axis_size(axis)
        forward = [(i, (i + 1) % count) for i in range(count)]
        backward = [(target, source) for source, target in forward]
        low = lax.ppermute(lax.slice_in_dim(block, block.shape[dim] - 1, None, axis=dim), axis, forward)
        high = lax.ppermute(lax.slice_in_dim(block, 0, 1, axis=dim), axis, backward)
        parts += [low, high]
    span_index = lax.axis_index("span")
    span_last = lax.axis_size("span") - 1
    parts[2] = parts[2] * (span_index != 0).astype(block.dtype)
    parts[3] = parts[3] * (span_index != span_last).astype(block.dtype)
    return parts


def stencil_kernel(j_ref, c_ref, cu_ref, cd_ref, su_ref, sd_ref, prev_ref, rate_ref, inlet_ref, out_ref):
    lane = lax.broadcasted_iota(jnp.int32, (8, 128), 1)
    probe = pltpu.roll(lane, 1, 1)
    numpy_order = probe == (lane + 127) % 128

    def chunk(i, carry):
        rows = pl.ds(pl.multiple_of(i * 8, 8), 8)
        cur = [c_ref[g, 0, rows, :] for g in range(NF)]
        cu = [cu_ref[g, 0, rows, :] for g in range(NF)]
        cd = [cd_ref[g, 0, rows, :] for g in range(NF)]
        su = [su_ref[g, 0, rows, :] for g in range(NF)]
        sd = [sd_ref[g, 0, rows, :] for g in range(NF)]
        au, ad = [], []
        for g in range(NF):
            one = pltpu.roll(cur[g], 1, 1)
            other = pltpu.roll(cur[g], 127, 1)
            down = jnp.where(numpy_order, one, other)
            up = jnp.where(numpy_order, other, one)
            ad.append(jnp.where(lane == 0, inlet_ref[g, 0, rows, :], down))
            au.append(jnp.where(lane == 127, 0.0, up))
        dc = [cu[g] - cd[g] for g in range(NF)]
        ds = [su[g] - sd[g] for g in range(NF)]
        da = [au[g] - ad[g] for g in range(NF)]
        rate = rate_ref[0, rows, :]
        for f in range(NF):
            convection = None
            for d, diff in enumerate((dc, ds, da)):
                term = j_ref[d * NF * NF + f * NF] * diff[0]
                for g in range(1, NF):
                    term = term + j_ref[d * NF * NF + f * NF + g] * diff[g]
                convection = term if convection is None else convection + term
            laplacian = cu[f] + cd[f] + (su[f] + sd[f]) + (au[f] + ad[f]) - 6.0 * cur[f]
            residual = (
                inv_step * (cur[f] - prev_ref[f, 0, rows, :])
                + 0.5 * convection
                - viscosity * laplacian
            )
            out_ref[f, 0, rows, :] = cur[f] - rate * residual
        return carry

    lax.fori_loop(0, c_ref.shape[2] // 8, chunk, 0)


def sweep(current, previous, rate_cells, inlet_column, jacobians, parts=None):
    if parts is None:
        parts = halo_parts(current)
    circ_low, circ_high, span_low, span_high = parts
    padded = jnp.concatenate([circ_low, current, circ_high], axis=1)
    span_up = jnp.concatenate([current[:, :, 1:], span_high], axis=2)
    span_down = jnp.concatenate([span_low, current[:, :, :-1]], axis=2)
    nf, rows, span, axial = current.shape
    block = (nf, 1, span, axial)
    spec = lambda shift: pl.BlockSpec(block, lambda t: (0, t + shift, 0, 0))
    out = pl.pallas_call(
        stencil_kernel,
        grid=(rows,),
        in_specs=[
            pl.BlockSpec(memory_space=pltpu.SMEM),
            spec(1),
            spec(2),
            spec(0),
            spec(0),
            spec(0),
            spec(0),
            pl.BlockSpec((1, span, axial), lambda t: (t, 0, 0)),
            pl.BlockSpec((nf, 1, span, 1), lambda t: (0, t, 0, 0)),
        ],
        out_specs=spec(0),
        out_shape=jax.ShapeDtypeStruct(current.shape, current.dtype),
    )(jacobians.reshape(-1), padded, padded, padded, span_up, span_down, previous, rate_cells, inlet_column)
    return out, parts


def contract(matrix, values):
    column = lambda g: matrix[:, g].reshape((-1,) + (1,) * (values.ndim - 1))
    total = column(0) * values[0][None]
    for g in range(1, matrix.shape[1]):
        total = total + column(g) * values[g][None]
    return total


def body(
    q_old, pseudo_rate, flux_jacobians, rotor_face, offsets, owners, slots, weight_idx, weight_table
):
    circ_count = lax.axis_size("circ")
    span_count = lax.axis_size("span")
    rows_local = rotor_face.shape[1]
    total_rows = rows_local * circ_count
    copies = jnp.broadcast_to(rotor_face[None], (circ_count,) + rotor_face.shape)
    gathered = lax.all_to_all(copies, "circ", 0, 0, tiled=True)
    row_iota = jnp.arange(rows_local, dtype=jnp.int32)
    first_row = lax.axis_index("circ") * rows_local
    source_rows = (first_row + row_iota[:, None] - offsets[None, :]) % total_rows
    global_rows = jnp.arange(total_rows, dtype=jnp.int32).reshape(circ_count, rows_local)
    picks = global_rows[:, None, :, None, None] == source_rows[None, None, None]
    rotated = jnp.sum(
        jnp.where(picks, gathered[:, :, :, None, :], 0.0), axis=(0, 2)
    )
    panels = rotated.reshape(NF, rows_local, KP_DEV, PW)
    table_ids = jnp.arange(weight_table.shape[0], dtype=jnp.int32)
    weights = jnp.sum(jnp.where(weight_idx[..., None] == table_ids, weight_table, 0.0), axis=-1)
    targets = owners[0] * KP_DEV + slots[0]
    local_weights = weights[0]
    panel_ids = jnp.arange(KP_DEV * span_count, dtype=jnp.int32)
    mixing = jnp.sum(
        jnp.where(targets[None] == panel_ids[:, None, None], local_weights[None], 0.0), axis=-1
    ).reshape(span_count, KP_DEV, KP_DEV)
    contributions = jnp.einsum(
        "ogk,ftkp->oftgp", mixing, panels, precision=lax.Precision.HIGHEST
    ).reshape(span_count, NF, rows_local, KP_DEV * PW)
    received = lax.all_to_all(contributions, "span", 0, 0, tiled=True)
    inlet_plane = jnp.sum(received, axis=0)

    inlet_column = inlet_plane[..., None]
    contributions, q_for_halo = lax.optimization_barrier((contributions, q_old))
    old_parts = halo_parts(q_for_halo)
    mid, _ = sweep(q_old, q_old, pseudo_rate, inlet_column, flux_jacobians, old_parts)
    mid_parts = halo_parts(mid)
    zero_parts = [jnp.zeros_like(p) for p in mid_parts]
    new, _ = sweep(mid, q_old, pseudo_rate, inlet_column, flux_jacobians, zero_parts)
    circ_low, circ_high, span_low, span_high = mid_parts
    eye = jnp.eye(NF, dtype=q_old.dtype)
    from_low = lambda d: 0.5 * flux_jacobians[d] + viscosity * eye
    from_high = lambda d: viscosity * eye - 0.5 * flux_jacobians[d]
    rate = pseudo_rate[None]
    rows, span = q_old.shape[1], q_old.shape[2]
    circ_terms = jnp.concatenate(
        [
            rate[:, :1] * contract(from_low(0), circ_low),
            jnp.zeros((NF, rows - 2) + q_old.shape[2:], q_old.dtype),
            rate[:, -1:] * contract(from_high(0), circ_high),
        ],
        axis=1,
    )
    span_terms = jnp.concatenate(
        [
            rate[:, :, :1] * contract(from_low(1), span_low),
            jnp.zeros((NF, rows, span - 2, q_old.shape[3]), q_old.dtype),
            rate[:, :, -1:] * contract(from_high(1), span_high),
        ],
        axis=2,
    )
    return new + circ_terms + span_terms


def solution(mesh):
    return jax.shard_map(
        body,
        mesh=mesh,
        in_specs=(
            P(None, "circ", "span", None),
            P("circ", "span", None),
            P(),
            P(None, "circ", "span"),
            P("span"),
            P("circ", "span", None),
            P("circ", "span", None),
            P("circ", "span", None),
            P(),
        ),
        out_specs=P(None, "circ", "span", None),
        check_vma=False,
    )
```

```python
import jax
import jax.numpy as jnp
from jax import lax
from jax.experimental import pallas as pl
from jax.experimental.pallas import tpu as pltpu
from jax.sharding import PartitionSpec as P

NF = 5
KP_DEV = 4
PW = 32


inv_step = 0.5
viscosity = 0.1


def halo_parts(block):
    parts = []
    for axis, dim in (("circ", 1), ("span", 2)):
        count = lax.axis_size(axis)
        forward = [(i, (i + 1) % count) for i in range(count)]
        backward = [(target, source) for source, target in forward]
        low = lax.ppermute(lax.slice_in_dim(block, block.shape[dim] - 1, None, axis=dim), axis, forward)
        high = lax.ppermute(lax.slice_in_dim(block, 0, 1, axis=dim), axis, backward)
        parts += [low, high]
    span_index = lax.axis_index("span")
    span_last = lax.axis_size("span") - 1
    parts[2] = parts[2] * (span_index != 0).astype(block.dtype)
    parts[3] = parts[3] * (span_index != span_last).astype(block.dtype)
    return parts


def halo_shapes(block):
    nf, rows, span, axial = block.shape
    shapes = [(nf, 1, span, axial)] * 2 + [(nf, rows, 1, axial)] * 2
    return [jnp.zeros(shape, block.dtype) for shape in shapes]


def stencil_kernel(j_ref, c_ref, cu_ref, cd_ref, su_ref, sd_ref, prev_ref, rate_ref, inlet_ref, out_ref):
    lane = lax.broadcasted_iota(jnp.int32, (8, 128), 1)
    probe = pltpu.roll(lane, 1, 1)
    numpy_order = probe == (lane + 127) % 128

    def chunk(i, carry):
        rows = pl.ds(pl.multiple_of(i * 8, 8), 8)
        cur = [c_ref[g, 0, rows, :] for g in range(NF)]
        cu = [cu_ref[g, 0, rows, :] for g in range(NF)]
        cd = [cd_ref[g, 0, rows, :] for g in range(NF)]
        su = [su_ref[g, 0, rows, :] for g in range(NF)]
        sd = [sd_ref[g, 0, rows, :] for g in range(NF)]
        au, ad = [], []
        for g in range(NF):
            one = pltpu.roll(cur[g], 1, 1)
            other = pltpu.roll(cur[g], 127, 1)
            down = jnp.where(numpy_order, one, other)
            up = jnp.where(numpy_order, other, one)
            ad.append(jnp.where(lane == 0, inlet_ref[g, 0, rows, :], down))
            au.append(jnp.where(lane == 127, 0.0, up))
        dc = [cu[g] - cd[g] for g in range(NF)]
        ds = [su[g] - sd[g] for g in range(NF)]
        da = [au[g] - ad[g] for g in range(NF)]
        rate = rate_ref[0, rows, :]
        for f in range(NF):
            convection = None
            for d, diff in enumerate((dc, ds, da)):
                term = j_ref[d * NF * NF + f * NF] * diff[0]
                for g in range(1, NF):
                    term = term + j_ref[d * NF * NF + f * NF + g] * diff[g]
                convection = term if convection is None else convection + term
            laplacian = cu[f] + cd[f] + (su[f] + sd[f]) + (au[f] + ad[f]) - 6.0 * cur[f]
            residual = (
                inv_step * (cur[f] - prev_ref[f, 0, rows, :])
                + 0.5 * convection
                - viscosity * laplacian
            )
            out_ref[f, 0, rows, :] = cur[f] - rate * residual
        return carry

    lax.fori_loop(0, c_ref.shape[2] // 8, chunk, 0)


def sweep(current, previous, rate_cells, inlet_column, jacobians, parts=None):
    if parts is None:
        parts = halo_parts(current)
    circ_low, circ_high, span_low, span_high = parts
    padded = jnp.concatenate([circ_low, current, circ_high], axis=1)
    span_up = jnp.concatenate([current[:, :, 1:], span_high], axis=2)
    span_down = jnp.concatenate([span_low, current[:, :, :-1]], axis=2)
    nf, rows, span, axial = current.shape
    block = (nf, 1, span, axial)
    spec = lambda shift: pl.BlockSpec(block, lambda t: (0, t + shift, 0, 0))
    out = pl.pallas_call(
        stencil_kernel,
        grid=(rows,),
        in_specs=[
            pl.BlockSpec(memory_space=pltpu.SMEM),
            spec(1),
            spec(2),
            spec(0),
            spec(0),
            spec(0),
            spec(0),
            pl.BlockSpec((1, span, axial), lambda t: (t, 0, 0)),
            pl.BlockSpec((nf, 1, span, 1), lambda t: (0, t, 0, 0)),
        ],
        out_specs=spec(0),
        out_shape=jax.ShapeDtypeStruct(current.shape, current.dtype),
    )(jacobians.reshape(-1), padded, padded, padded, span_up, span_down, previous, rate_cells, inlet_column)
    return out, parts


def contract(matrix, values):
    column = lambda g: matrix[:, g].reshape((-1,) + (1,) * (values.ndim - 1))
    total = column(0) * values[0][None]
    for g in range(1, matrix.shape[1]):
        total = total + column(g) * values[g][None]
    return total


def body(
    q_old, pseudo_rate, flux_jacobians, rotor_face, offsets, owners, slots, weight_idx, weight_table
):
    circ_count = lax.axis_size("circ")
    span_count = lax.axis_size("span")
    rows_local = rotor_face.shape[1]
    total_rows = rows_local * circ_count
    copies = jnp.broadcast_to(rotor_face[None], (circ_count,) + rotor_face.shape)
    gathered = lax.all_to_all(copies, "circ", 0, 0, tiled=True)
    row_iota = jnp.arange(rows_local, dtype=jnp.int32)
    first_row = lax.axis_index("circ") * rows_local
    source_rows = (first_row + row_iota[:, None] - offsets[None, :]) % total_rows
    global_rows = jnp.arange(total_rows, dtype=jnp.int32).reshape(circ_count, rows_local)
    picks = global_rows[:, None, :, None, None] == source_rows[None, None, None]
    rotated = jnp.sum(
        jnp.where(picks, gathered[:, :, :, None, :], 0.0), axis=(0, 2)
    )
    panels = rotated.reshape(NF, rows_local, KP_DEV, PW)
    table_ids = jnp.arange(weight_table.shape[0], dtype=jnp.int32)
    weights = jnp.sum(jnp.where(weight_idx[..., None] == table_ids, weight_table, 0.0), axis=-1)
    targets = owners[0] * KP_DEV + slots[0]
    local_weights = weights[0]
    panel_ids = jnp.arange(KP_DEV * span_count, dtype=jnp.int32)
    mixing = jnp.sum(
        jnp.where(targets[None] == panel_ids[:, None, None], local_weights[None], 0.0), axis=-1
    ).reshape(span_count, KP_DEV, KP_DEV)
    contributions = jnp.einsum(
        "ogk,ftkp->oftgp", mixing, panels, precision=lax.Precision.HIGHEST
    ).reshape(span_count, NF, rows_local, KP_DEV * PW)
    received = lax.all_to_all(contributions, "span", 0, 0, tiled=True)
    inlet_plane = jnp.sum(received, axis=0)

    inlet_column = inlet_plane[..., None]
    zero_parts = halo_shapes(q_old)
    mid, _ = sweep(q_old, q_old, pseudo_rate, inlet_column, flux_jacobians, zero_parts)
    mid, q_for_halo = lax.optimization_barrier((mid, q_old))
    mid = mid + boundary_terms(halo_parts(q_for_halo), pseudo_rate, flux_jacobians)
    new, _ = sweep(mid, q_old, pseudo_rate, inlet_column, flux_jacobians, zero_parts)
    new, mid_for_halo = lax.optimization_barrier((new, mid))
    return new + boundary_terms(halo_parts(mid_for_halo), pseudo_rate, flux_jacobians)


def boundary_terms(parts, rate_cells, jacobians):
    circ_low, circ_high, span_low, span_high = parts
    nf, _, span, axial = circ_low.shape
    rows = span_low.shape[1]
    eye = jnp.eye(nf, dtype=circ_low.dtype)
    from_low = lambda d: 0.5 * jacobians[d] + viscosity * eye
    from_high = lambda d: viscosity * eye - 0.5 * jacobians[d]
    rate = rate_cells[None]
    circ_terms = jnp.concatenate(
        [
            rate[:, :1] * contract(from_low(0), circ_low),
            jnp.zeros((nf, rows - 2, span, axial), circ_low.dtype),
            rate[:, -1:] * contract(from_high(0), circ_high),
        ],
        axis=1,
    )
    span_terms = jnp.concatenate(
        [
            rate[:, :, :1] * contract(from_low(1), span_low),
            jnp.zeros((nf, rows, span - 2, axial), circ_low.dtype),
            rate[:, :, -1:] * contract(from_high(1), span_high),
        ],
        axis=2,
    )
    return circ_terms + span_terms


def solution(mesh):
    return jax.shard_map(
        body,
        mesh=mesh,
        in_specs=(
            P(None, "circ", "span", None),
            P("circ", "span", None),
            P(),
            P(None, "circ", "span"),
            P("span"),
            P("circ", "span", None),
            P("circ", "span", None),
            P("circ", "span", None),
            P(),
        ),
        out_specs=P(None, "circ", "span", None),
        check_vma=False,
    )
```

```python
import jax
import jax.numpy as jnp
from jax import lax
from jax.experimental import pallas as pl
from jax.experimental.pallas import tpu as pltpu
from jax.sharding import PartitionSpec as P

NF = 5
KP_DEV = 4
PW = 32
CAP = 2


inv_step = 0.5
viscosity = 0.1


def with_halo(block, sides, width):
    for axis, dim in sides:
        count = lax.axis_size(axis)
        forward = [(i, i + 1) for i in range(count - 1)]
        forward.append((count - 1, 0))
        backward = [(target, source) for source, target in forward]
        low = lax.ppermute(
            lax.slice_in_dim(block, block.shape[dim] - width, None, axis=dim), axis, forward
        )
        high = lax.ppermute(lax.slice_in_dim(block, 0, width, axis=dim), axis, backward)
        block = jnp.concatenate([low, block, high], axis=dim)
    return block


def halo_parts(block):
    parts = []
    for axis, dim in (("circ", 1), ("span", 2)):
        count = lax.axis_size(axis)
        forward = [(i, (i + 1) % count) for i in range(count)]
        backward = [(target, source) for source, target in forward]
        low = lax.ppermute(lax.slice_in_dim(block, block.shape[dim] - 1, None, axis=dim), axis, forward)
        high = lax.ppermute(lax.slice_in_dim(block, 0, 1, axis=dim), axis, backward)
        parts += [low, high]
    span_index = lax.axis_index("span")
    span_last = lax.axis_size("span") - 1
    parts[2] = parts[2] * (span_index != 0).astype(block.dtype)
    parts[3] = parts[3] * (span_index != span_last).astype(block.dtype)
    return parts


def lateral_of(block, parts):
    circ_low, circ_high, span_low, span_high = parts
    return (
        jnp.concatenate([block[:, 1:], circ_high], axis=1),
        jnp.concatenate([circ_low, block[:, :-1]], axis=1),
        jnp.concatenate([block[:, :, 1:], span_high], axis=2),
        jnp.concatenate([span_low, block[:, :, :-1]], axis=2),
    )


def stencil_kernel(j_ref, c_ref, cu_ref, cd_ref, su_ref, sd_ref, prev_ref, rate_ref, inlet_ref, out_ref):
    lane = lax.broadcasted_iota(jnp.int32, (8, 128), 1)
    probe = pltpu.roll(lane, 1, 1)
    numpy_order = probe == (lane + 127) % 128

    def chunk(i, carry):
        rows = pl.ds(pl.multiple_of(i * 8, 8), 8)
        cur = [c_ref[g, 0, rows, :] for g in range(NF)]
        cu = [cu_ref[g, 0, rows, :] for g in range(NF)]
        cd = [cd_ref[g, 0, rows, :] for g in range(NF)]
        su = [su_ref[g, 0, rows, :] for g in range(NF)]
        sd = [sd_ref[g, 0, rows, :] for g in range(NF)]
        au, ad = [], []
        for g in range(NF):
            one = pltpu.roll(cur[g], 1, 1)
            other = pltpu.roll(cur[g], 127, 1)
            down = jnp.where(numpy_order, one, other)
            up = jnp.where(numpy_order, other, one)
            ad.append(jnp.where(lane == 0, inlet_ref[g, 0, rows, :], down))
            au.append(jnp.where(lane == 127, 0.0, up))
        dc = [cu[g] - cd[g] for g in range(NF)]
        ds = [su[g] - sd[g] for g in range(NF)]
        da = [au[g] - ad[g] for g in range(NF)]
        rate = rate_ref[0, rows, :]
        for f in range(NF):
            convection = None
            for d, diff in enumerate((dc, ds, da)):
                term = j_ref[d * NF * NF + f * NF] * diff[0]
                for g in range(1, NF):
                    term = term + j_ref[d * NF * NF + f * NF + g] * diff[g]
                convection = term if convection is None else convection + term
            laplacian = cu[f] + cd[f] + (su[f] + sd[f]) + (au[f] + ad[f]) - 6.0 * cur[f]
            residual = (
                inv_step * (cur[f] - prev_ref[f, 0, rows, :])
                + 0.5 * convection
                - viscosity * laplacian
            )
            out_ref[f, 0, rows, :] = cur[f] - rate * residual
        return carry

    lax.fori_loop(0, c_ref.shape[2] // 8, chunk, 0)


def sweep(current, previous, rate_cells, inlet_column, jacobians):
    parts = halo_parts(current)
    circ_low, circ_high, span_low, span_high = parts
    padded = jnp.concatenate([circ_low, current, circ_high], axis=1)
    span_up = jnp.concatenate([current[:, :, 1:], span_high], axis=2)
    span_down = jnp.concatenate([span_low, current[:, :, :-1]], axis=2)
    nf, rows, span, axial = current.shape
    block = (nf, 1, span, axial)
    spec = lambda shift: pl.BlockSpec(block, lambda t: (0, t + shift, 0, 0))
    out = pl.pallas_call(
        stencil_kernel,
        grid=(rows,),
        in_specs=[
            pl.BlockSpec(memory_space=pltpu.SMEM),
            spec(1),
            spec(2),
            spec(0),
            spec(0),
            spec(0),
            spec(0),
            pl.BlockSpec((1, span, axial), lambda t: (t, 0, 0)),
            pl.BlockSpec((nf, 1, span, 1), lambda t: (0, t, 0, 0)),
        ],
        out_specs=spec(0),
        out_shape=jax.ShapeDtypeStruct(current.shape, current.dtype),
    )(jacobians.reshape(-1), padded, padded, padded, span_up, span_down, previous, rate_cells, inlet_column)
    return out, parts


def contract(matrix, values):
    column = lambda g: matrix[:, g].reshape((-1,) + (1,) * (values.ndim - 1))
    total = column(0) * values[0][None]
    for g in range(1, matrix.shape[1]):
        total = total + column(g) * values[g][None]
    return total


def update(current, previous, rate_cells, neighbours, jacobians):
    circ_up, circ_down, span_up, span_down, axial_up, axial_down = neighbours
    convection = contract(jacobians[0], circ_up - circ_down)
    convection = convection + contract(jacobians[1], span_up - span_down)
    convection = convection + contract(jacobians[2], axial_up - axial_down)
    laplacian = (
        circ_up + circ_down + (span_up + span_down) + (axial_up + axial_down) - 6.0 * current
    )
    residual = inv_step * (current - previous) + 0.5 * convection - viscosity * laplacian
    return current - rate_cells[None] * residual


def lateral(padded):
    return (
        padded[:, 2:, 1:-1],
        padded[:, :-2, 1:-1],
        padded[:, 1:-1, 2:],
        padded[:, 1:-1, :-2],
    )


def advance(padded, current, previous, rate_cells, jacobians):
    zero_column = jnp.zeros_like(current[..., :1])
    axial_up = jnp.concatenate([current[..., 1:], zero_column], axis=-1)
    axial_down = jnp.concatenate([zero_column, current[..., :-1]], axis=-1)
    neighbours = lateral(padded) + (axial_up, axial_down)
    return update(current, previous, rate_cells, neighbours, jacobians)


def wall_zero(field_array, width):
    span_index = lax.axis_index("span")
    span_count = lax.axis_size("span")
    length = field_array.shape[2]
    position = jnp.arange(length, dtype=jnp.int32)
    at_hub = jnp.logical_and(span_index == 0, position < width)
    at_tip = jnp.logical_and(span_index == span_count - 1, position >= length - width)
    keeping = jnp.logical_not(jnp.logical_or(at_hub, at_tip)).astype(field_array.dtype)
    keeping = keeping.reshape(1, 1, length, 1)
    return field_array * keeping


def body(
    q_old, pseudo_rate, flux_jacobians, rotor_face, offsets, owners, slots, weight_idx, weight_table
):
    circ_count = lax.axis_size("circ")
    span_count = lax.axis_size("span")
    rows_local = rotor_face.shape[1]
    total_rows = rows_local * circ_count
    copies = jnp.broadcast_to(rotor_face[None], (circ_count,) + rotor_face.shape)
    gathered = lax.all_to_all(copies, "circ", 0, 0, tiled=True)
    row_iota = jnp.arange(rows_local, dtype=jnp.int32)
    first_row = lax.axis_index("circ") * rows_local
    source_rows = (first_row + row_iota[:, None] - offsets[None, :]) % total_rows
    global_rows = jnp.arange(total_rows, dtype=jnp.int32).reshape(circ_count, rows_local)
    picks = global_rows[:, None, :, None, None] == source_rows[None, None, None]
    rotated = jnp.sum(
        jnp.where(picks, gathered[:, :, :, None, :], 0.0), axis=(0, 2)
    )
    panels = rotated.reshape(NF, rows_local, KP_DEV, PW)
    table_ids = jnp.arange(weight_table.shape[0], dtype=jnp.int32)
    weights = jnp.sum(jnp.where(weight_idx[..., None] == table_ids, weight_table, 0.0), axis=-1)
    owner_of = owners[0].reshape(-1)
    slot_of = slots[0].reshape(-1)
    weight_of = weights[0].reshape(-1)
    entries = owner_of.shape[0]
    panel_of = jnp.arange(entries, dtype=jnp.int32) // owners.shape[-1]
    earlier = jnp.tril(jnp.ones((entries, entries), dtype=bool), -1)
    position = jnp.sum(earlier & (owner_of[:, None] == owner_of[None, :]), axis=1)
    chosen = (owner_of[None, None] == jnp.arange(span_count, dtype=jnp.int32)[:, None, None]) & (
        position[None, None] == jnp.arange(CAP, dtype=jnp.int32)[None, :, None]
    )
    picked = jnp.where(chosen, weight_of, 0.0)
    selection = jnp.sum(
        picked[..., None] * (panel_of[:, None] == jnp.arange(KP_DEV, dtype=jnp.int32)), axis=2
    )
    data = jnp.einsum("opk,ftkq->opftq", selection, panels, precision=lax.Precision.HIGHEST)
    code = jnp.sum(jnp.where(chosen, slot_of + 1, 0), axis=2).astype(jnp.float32) - 1.0
    payload = jnp.concatenate(
        [data.reshape(span_count, CAP, -1), code[..., None]], axis=-1
    )
    received = lax.all_to_all(payload, "span", 0, 0, tiled=True)
    values = received[..., :-1].reshape(span_count * CAP, NF, rows_local, 1, PW)
    codes = received[..., -1].reshape(span_count * CAP, 1, 1, 1, 1)
    slot_ids = jnp.arange(KP_DEV, dtype=jnp.float32).reshape(1, 1, 1, KP_DEV, 1)
    inlet_plane = jnp.sum(jnp.where(codes == slot_ids, values, 0.0), axis=0).reshape(
        NF, rows_local, KP_DEV * PW
    )

    inlet_column = inlet_plane[..., None]
    mid, _ = sweep(q_old, q_old, pseudo_rate, inlet_column, flux_jacobians)
    new, _ = sweep(mid, q_old, pseudo_rate, inlet_column, flux_jacobians)
    return new


def solution(mesh):
    return jax.shard_map(
        body,
        mesh=mesh,
        in_specs=(
            P(None, "circ", "span", None),
            P("circ", "span", None),
            P(),
            P(None, "circ", "span"),
            P("span"),
            P("circ", "span", None),
            P("circ", "span", None),
            P("circ", "span", None),
            P(),
        ),
        out_specs=P(None, "circ", "span", None),
        check_vma=False,
    )
```

```python
import jax
import jax.numpy as jnp
from jax import lax
from jax.experimental import pallas as pl
from jax.experimental.pallas import tpu as pltpu
from jax.sharding import PartitionSpec as P

NF = 5
KP_DEV = 4
PW = 32
CAP = 2


inv_step = 0.5
viscosity = 0.1


def with_halo(block, sides, width):
    for axis, dim in sides:
        count = lax.axis_size(axis)
        forward = [(i, i + 1) for i in range(count - 1)]
        forward.append((count - 1, 0))
        backward = [(target, source) for source, target in forward]
        low = lax.ppermute(
            lax.slice_in_dim(block, block.shape[dim] - width, None, axis=dim), axis, forward
        )
        high = lax.ppermute(lax.slice_in_dim(block, 0, width, axis=dim), axis, backward)
        block = jnp.concatenate([low, block, high], axis=dim)
    return block


def halo_parts(block):
    parts = []
    for axis, dim in (("circ", 1), ("span", 2)):
        count = lax.axis_size(axis)
        forward = [(i, (i + 1) % count) for i in range(count)]
        backward = [(target, source) for source, target in forward]
        low = lax.ppermute(lax.slice_in_dim(block, block.shape[dim] - 1, None, axis=dim), axis, forward)
        high = lax.ppermute(lax.slice_in_dim(block, 0, 1, axis=dim), axis, backward)
        parts += [low, high]
    span_index = lax.axis_index("span")
    span_last = lax.axis_size("span") - 1
    parts[2] = parts[2] * (span_index != 0).astype(block.dtype)
    parts[3] = parts[3] * (span_index != span_last).astype(block.dtype)
    return parts


def lateral_of(block, parts):
    circ_low, circ_high, span_low, span_high = parts
    return (
        jnp.concatenate([block[:, 1:], circ_high], axis=1),
        jnp.concatenate([circ_low, block[:, :-1]], axis=1),
        jnp.concatenate([block[:, :, 1:], span_high], axis=2),
        jnp.concatenate([span_low, block[:, :, :-1]], axis=2),
    )


def stencil_kernel(
    j_ref, c_ref, cu_ref, cd_ref, su_ref, sd_ref, prev_ref, rate_ref, inlet_ref, out_ref, inlet_scr
):
    span, axial = inlet_scr.shape[1:]
    for g in range(NF):
        row = inlet_ref[0, g : g + 1, :]
        inlet_scr[g] = jnp.transpose(jnp.broadcast_to(row, (axial, span)))
    lane = lax.broadcasted_iota(jnp.int32, (8, 128), 1)
    probe = pltpu.roll(lane, 1, 1)
    numpy_order = probe == (lane + 127) % 128

    def chunk(i, carry):
        rows = pl.ds(pl.multiple_of(i * 8, 8), 8)
        cur = [c_ref[g, 0, rows, :] for g in range(NF)]
        cu = [cu_ref[g, 0, rows, :] for g in range(NF)]
        cd = [cd_ref[g, 0, rows, :] for g in range(NF)]
        su = [su_ref[g, 0, rows, :] for g in range(NF)]
        sd = [sd_ref[g, 0, rows, :] for g in range(NF)]
        au, ad = [], []
        for g in range(NF):
            one = pltpu.roll(cur[g], 1, 1)
            other = pltpu.roll(cur[g], 127, 1)
            down = jnp.where(numpy_order, one, other)
            up = jnp.where(numpy_order, other, one)
            ad.append(jnp.where(lane == 0, inlet_scr[g, rows, :], down))
            au.append(jnp.where(lane == 127, 0.0, up))
        dc = [cu[g] - cd[g] for g in range(NF)]
        ds = [su[g] - sd[g] for g in range(NF)]
        da = [au[g] - ad[g] for g in range(NF)]
        rate = rate_ref[0, rows, :]
        for f in range(NF):
            convection = None
            for d, diff in enumerate((dc, ds, da)):
                term = j_ref[d * NF * NF + f * NF] * diff[0]
                for g in range(1, NF):
                    term = term + j_ref[d * NF * NF + f * NF + g] * diff[g]
                convection = term if convection is None else convection + term
            laplacian = cu[f] + cd[f] + (su[f] + sd[f]) + (au[f] + ad[f]) - 6.0 * cur[f]
            residual = (
                inv_step * (cur[f] - prev_ref[f, 0, rows, :])
                + 0.5 * convection
                - viscosity * laplacian
            )
            out_ref[f, 0, rows, :] = cur[f] - rate * residual
        return carry

    lax.fori_loop(0, c_ref.shape[2] // 8, chunk, 0)


def sweep(current, previous, rate_cells, inlet_rows, jacobians):
    parts = halo_parts(current)
    circ_low, circ_high, span_low, span_high = parts
    padded = jnp.concatenate([circ_low, current, circ_high], axis=1)
    span_up = jnp.concatenate([current[:, :, 1:], span_high], axis=2)
    span_down = jnp.concatenate([span_low, current[:, :, :-1]], axis=2)
    nf, rows, span, axial = current.shape
    block = (nf, 1, span, axial)
    spec = lambda shift: pl.BlockSpec(block, lambda t: (0, t + shift, 0, 0))
    out = pl.pallas_call(
        stencil_kernel,
        grid=(rows,),
        in_specs=[
            pl.BlockSpec(memory_space=pltpu.SMEM),
            spec(1),
            spec(2),
            spec(0),
            spec(0),
            spec(0),
            spec(0),
            pl.BlockSpec((1, span, axial), lambda t: (t, 0, 0)),
            pl.BlockSpec((1, nf, span), lambda t: (t, 0, 0)),
        ],
        scratch_shapes=[pltpu.VMEM((nf, span, axial), current.dtype)],
        out_specs=spec(0),
        out_shape=jax.ShapeDtypeStruct(current.shape, current.dtype),
    )(jacobians.reshape(-1), padded, padded, padded, span_up, span_down, previous, rate_cells, inlet_rows)
    return out, parts


def contract(matrix, values):
    column = lambda g: matrix[:, g].reshape((-1,) + (1,) * (values.ndim - 1))
    total = column(0) * values[0][None]
    for g in range(1, matrix.shape[1]):
        total = total + column(g) * values[g][None]
    return total


def update(current, previous, rate_cells, neighbours, jacobians):
    circ_up, circ_down, span_up, span_down, axial_up, axial_down = neighbours
    convection = contract(jacobians[0], circ_up - circ_down)
    convection = convection + contract(jacobians[1], span_up - span_down)
    convection = convection + contract(jacobians[2], axial_up - axial_down)
    laplacian = (
        circ_up + circ_down + (span_up + span_down) + (axial_up + axial_down) - 6.0 * current
    )
    residual = inv_step * (current - previous) + 0.5 * convection - viscosity * laplacian
    return current - rate_cells[None] * residual


def lateral(padded):
    return (
        padded[:, 2:, 1:-1],
        padded[:, :-2, 1:-1],
        padded[:, 1:-1, 2:],
        padded[:, 1:-1, :-2],
    )


def advance(padded, current, previous, rate_cells, jacobians):
    zero_column = jnp.zeros_like(current[..., :1])
    axial_up = jnp.concatenate([current[..., 1:], zero_column], axis=-1)
    axial_down = jnp.concatenate([zero_column, current[..., :-1]], axis=-1)
    neighbours = lateral(padded) + (axial_up, axial_down)
    return update(current, previous, rate_cells, neighbours, jacobians)


def wall_zero(field_array, width):
    span_index = lax.axis_index("span")
    span_count = lax.axis_size("span")
    length = field_array.shape[2]
    position = jnp.arange(length, dtype=jnp.int32)
    at_hub = jnp.logical_and(span_index == 0, position < width)
    at_tip = jnp.logical_and(span_index == span_count - 1, position >= length - width)
    keeping = jnp.logical_not(jnp.logical_or(at_hub, at_tip)).astype(field_array.dtype)
    keeping = keeping.reshape(1, 1, length, 1)
    return field_array * keeping


def body(
    q_old, pseudo_rate, flux_jacobians, rotor_face, offsets, owners, slots, weight_idx, weight_table
):
    circ_count = lax.axis_size("circ")
    span_count = lax.axis_size("span")
    rows_local = rotor_face.shape[1]
    total_rows = rows_local * circ_count
    copies = jnp.broadcast_to(rotor_face[None], (circ_count,) + rotor_face.shape)
    gathered = lax.all_to_all(copies, "circ", 0, 0, tiled=True)
    row_iota = jnp.arange(rows_local, dtype=jnp.int32)
    first_row = lax.axis_index("circ") * rows_local
    source_rows = (first_row + row_iota[:, None] - offsets[None, :]) % total_rows
    global_rows = jnp.arange(total_rows, dtype=jnp.int32).reshape(circ_count, rows_local)
    picks = global_rows[:, None, :, None, None] == source_rows[None, None, None]
    rotated = jnp.sum(
        jnp.where(picks, gathered[:, :, :, None, :], 0.0), axis=(0, 2)
    )
    panels = rotated.reshape(NF, rows_local, KP_DEV, PW)
    table_ids = jnp.arange(weight_table.shape[0], dtype=jnp.int32)
    weights = jnp.sum(jnp.where(weight_idx[..., None] == table_ids, weight_table, 0.0), axis=-1)
    owner_of = owners[0].reshape(-1)
    slot_of = slots[0].reshape(-1)
    weight_of = weights[0].reshape(-1)
    entries = owner_of.shape[0]
    panel_of = jnp.arange(entries, dtype=jnp.int32) // owners.shape[-1]
    earlier = jnp.tril(jnp.ones((entries, entries), dtype=bool), -1)
    position = jnp.sum(earlier & (owner_of[:, None] == owner_of[None, :]), axis=1)
    chosen = (owner_of[None, None] == jnp.arange(span_count, dtype=jnp.int32)[:, None, None]) & (
        position[None, None] == jnp.arange(CAP, dtype=jnp.int32)[None, :, None]
    )
    picked = jnp.where(chosen, weight_of, 0.0)
    selection = jnp.sum(
        picked[..., None] * (panel_of[:, None] == jnp.arange(KP_DEV, dtype=jnp.int32)), axis=2
    )
    data = jnp.einsum("opk,ftkq->opftq", selection, panels, precision=lax.Precision.HIGHEST)
    code = jnp.sum(jnp.where(chosen, slot_of + 1, 0), axis=2).astype(jnp.float32) - 1.0
    payload = jnp.concatenate(
        [data.reshape(span_count, CAP, -1), code[..., None]], axis=-1
    )
    received = lax.all_to_all(payload, "span", 0, 0, tiled=True)
    values = received[..., :-1].reshape(span_count * CAP, NF, rows_local, 1, PW)
    codes = received[..., -1].reshape(span_count * CAP, 1, 1, 1, 1)
    slot_ids = jnp.arange(KP_DEV, dtype=jnp.float32).reshape(1, 1, 1, KP_DEV, 1)
    inlet_rows = jnp.transpose(
        jnp.sum(jnp.where(codes == slot_ids, values, 0.0), axis=0), (1, 0, 2, 3)
    ).reshape(rows_local, NF, KP_DEV * PW)

    mid, _ = sweep(q_old, q_old, pseudo_rate, inlet_rows, flux_jacobians)
    new, _ = sweep(mid, q_old, pseudo_rate, inlet_rows, flux_jacobians)
    return new


def solution(mesh):
    return jax.shard_map(
        body,
        mesh=mesh,
        in_specs=(
            P(None, "circ", "span", None),
            P("circ", "span", None),
            P(),
            P(None, "circ", "span"),
            P("span"),
            P("circ", "span", None),
            P("circ", "span", None),
            P("circ", "span", None),
            P(),
        ),
        out_specs=P(None, "circ", "span", None),
        check_vma=False,
    )
```

```python
import jax
import jax.numpy as jnp
from jax import lax
from jax.experimental import pallas as pl
from jax.experimental.pallas import tpu as pltpu
from jax.sharding import PartitionSpec as P

NF = 5
KP_DEV = 4
PW = 32
CAP = 2


inv_step = 0.5
viscosity = 0.1


def with_halo(block, sides, width):
    for axis, dim in sides:
        count = lax.axis_size(axis)
        forward = [(i, i + 1) for i in range(count - 1)]
        forward.append((count - 1, 0))
        backward = [(target, source) for source, target in forward]
        low = lax.ppermute(
            lax.slice_in_dim(block, block.shape[dim] - width, None, axis=dim), axis, forward
        )
        high = lax.ppermute(lax.slice_in_dim(block, 0, width, axis=dim), axis, backward)
        block = jnp.concatenate([low, block, high], axis=dim)
    return block


def halo_parts(block, span_edges=None):
    parts = []
    for axis, dim in (("circ", 1), ("span", 2)):
        if dim == 2 and span_edges is not None:
            count = lax.axis_size(axis)
            forward = [(i, (i + 1) % count) for i in range(count)]
            backward = [(target, source) for source, target in forward]
            parts += [
                lax.ppermute(span_edges[1], axis, forward),
                lax.ppermute(span_edges[0], axis, backward),
            ]
            continue
        count = lax.axis_size(axis)
        forward = [(i, (i + 1) % count) for i in range(count)]
        backward = [(target, source) for source, target in forward]
        low = lax.ppermute(lax.slice_in_dim(block, block.shape[dim] - 1, None, axis=dim), axis, forward)
        high = lax.ppermute(lax.slice_in_dim(block, 0, 1, axis=dim), axis, backward)
        parts += [low, high]
    span_index = lax.axis_index("span")
    span_last = lax.axis_size("span") - 1
    parts[2] = parts[2] * (span_index != 0).astype(block.dtype)
    parts[3] = parts[3] * (span_index != span_last).astype(block.dtype)
    return parts


def lateral_of(block, parts):
    circ_low, circ_high, span_low, span_high = parts
    return (
        jnp.concatenate([block[:, 1:], circ_high], axis=1),
        jnp.concatenate([circ_low, block[:, :-1]], axis=1),
        jnp.concatenate([block[:, :, 1:], span_high], axis=2),
        jnp.concatenate([span_low, block[:, :, :-1]], axis=2),
    )


def stencil_kernel(
    j_ref, c_ref, cu_ref, cd_ref, su_ref, sd_ref, prev_ref, rate_ref, inlet_ref,
    out_ref, first_ref, last_ref, inlet_scr,
):
    span, axial = inlet_scr.shape[1:]
    for g in range(NF):
        row = inlet_ref[0, g : g + 1, :]
        inlet_scr[g] = jnp.transpose(jnp.broadcast_to(row, (axial, span)))
    lane = lax.broadcasted_iota(jnp.int32, (8, 128), 1)
    probe = pltpu.roll(lane, 1, 1)
    numpy_order = probe == (lane + 127) % 128

    def chunk(i, carry):
        rows = pl.ds(pl.multiple_of(i * 8, 8), 8)
        cur = [c_ref[g, 0, rows, :] for g in range(NF)]
        cu = [cu_ref[g, 0, rows, :] for g in range(NF)]
        cd = [cd_ref[g, 0, rows, :] for g in range(NF)]
        su = [su_ref[g, 0, rows, :] for g in range(NF)]
        sd = [sd_ref[g, 0, rows, :] for g in range(NF)]
        au, ad = [], []
        for g in range(NF):
            one = pltpu.roll(cur[g], 1, 1)
            other = pltpu.roll(cur[g], 127, 1)
            down = jnp.where(numpy_order, one, other)
            up = jnp.where(numpy_order, other, one)
            ad.append(jnp.where(lane == 0, inlet_scr[g, rows, :], down))
            au.append(jnp.where(lane == 127, 0.0, up))
        dc = [cu[g] - cd[g] for g in range(NF)]
        ds = [su[g] - sd[g] for g in range(NF)]
        da = [au[g] - ad[g] for g in range(NF)]
        rate = rate_ref[0, rows, :]
        for f in range(NF):
            convection = None
            for d, diff in enumerate((dc, ds, da)):
                term = j_ref[d * NF * NF + f * NF] * diff[0]
                for g in range(1, NF):
                    term = term + j_ref[d * NF * NF + f * NF + g] * diff[g]
                convection = term if convection is None else convection + term
            laplacian = cu[f] + cd[f] + (su[f] + sd[f]) + (au[f] + ad[f]) - 6.0 * cur[f]
            residual = (
                inv_step * (cur[f] - prev_ref[f, 0, rows, :])
                + 0.5 * convection
                - viscosity * laplacian
            )
            value = cur[f] - rate * residual
            out_ref[f, 0, rows, :] = value

            @pl.when(i == 0)
            def _():
                first_ref[f, 0, 0:1, :] = value[0:1]

            @pl.when(i == chunks - 1)
            def _():
                last_ref[f, 0, 0:1, :] = value[7:8]

        return carry

    chunks = c_ref.shape[2] // 8
    lax.fori_loop(0, chunks, chunk, 0)


def sweep(current, previous, rate_cells, inlet_rows, jacobians, parts=None):
    if parts is None:
        parts = halo_parts(current)
    circ_low, circ_high, span_low, span_high = parts
    padded = jnp.concatenate([circ_low, current, circ_high], axis=1)
    span_up = jnp.concatenate([current[:, :, 1:], span_high], axis=2)
    span_down = jnp.concatenate([span_low, current[:, :, :-1]], axis=2)
    nf, rows, span, axial = current.shape
    block = (nf, 1, span, axial)
    spec = lambda shift: pl.BlockSpec(block, lambda t: (0, t + shift, 0, 0))
    out = pl.pallas_call(
        stencil_kernel,
        grid=(rows,),
        in_specs=[
            pl.BlockSpec(memory_space=pltpu.SMEM),
            spec(1),
            spec(2),
            spec(0),
            spec(0),
            spec(0),
            spec(0),
            pl.BlockSpec((1, span, axial), lambda t: (t, 0, 0)),
            pl.BlockSpec((1, nf, span), lambda t: (t, 0, 0)),
        ],
        scratch_shapes=[pltpu.VMEM((nf, span, axial), current.dtype)],
        out_specs=[spec(0)] + [pl.BlockSpec((nf, 1, 1, axial), lambda t: (0, t, 0, 0))] * 2,
        out_shape=[jax.ShapeDtypeStruct(current.shape, current.dtype)]
        + [jax.ShapeDtypeStruct((nf, rows, 1, axial), current.dtype)] * 2,
    )(jacobians.reshape(-1), padded, padded, padded, span_up, span_down, previous, rate_cells, inlet_rows)
    out, first, last = out
    return out, (first, last)


def contract(matrix, values):
    column = lambda g: matrix[:, g].reshape((-1,) + (1,) * (values.ndim - 1))
    total = column(0) * values[0][None]
    for g in range(1, matrix.shape[1]):
        total = total + column(g) * values[g][None]
    return total


def update(current, previous, rate_cells, neighbours, jacobians):
    circ_up, circ_down, span_up, span_down, axial_up, axial_down = neighbours
    convection = contract(jacobians[0], circ_up - circ_down)
    convection = convection + contract(jacobians[1], span_up - span_down)
    convection = convection + contract(jacobians[2], axial_up - axial_down)
    laplacian = (
        circ_up + circ_down + (span_up + span_down) + (axial_up + axial_down) - 6.0 * current
    )
    residual = inv_step * (current - previous) + 0.5 * convection - viscosity * laplacian
    return current - rate_cells[None] * residual


def lateral(padded):
    return (
        padded[:, 2:, 1:-1],
        padded[:, :-2, 1:-1],
        padded[:, 1:-1, 2:],
        padded[:, 1:-1, :-2],
    )


def advance(padded, current, previous, rate_cells, jacobians):
    zero_column = jnp.zeros_like(current[..., :1])
    axial_up = jnp.concatenate([current[..., 1:], zero_column], axis=-1)
    axial_down = jnp.concatenate([zero_column, current[..., :-1]], axis=-1)
    neighbours = lateral(padded) + (axial_up, axial_down)
    return update(current, previous, rate_cells, neighbours, jacobians)


def wall_zero(field_array, width):
    span_index = lax.axis_index("span")
    span_count = lax.axis_size("span")
    length = field_array.shape[2]
    position = jnp.arange(length, dtype=jnp.int32)
    at_hub = jnp.logical_and(span_index == 0, position < width)
    at_tip = jnp.logical_and(span_index == span_count - 1, position >= length - width)
    keeping = jnp.logical_not(jnp.logical_or(at_hub, at_tip)).astype(field_array.dtype)
    keeping = keeping.reshape(1, 1, length, 1)
    return field_array * keeping


def body(
    q_old, pseudo_rate, flux_jacobians, rotor_face, offsets, owners, slots, weight_idx, weight_table
):
    circ_count = lax.axis_size("circ")
    span_count = lax.axis_size("span")
    rows_local = rotor_face.shape[1]
    total_rows = rows_local * circ_count
    copies = jnp.broadcast_to(rotor_face[None], (circ_count,) + rotor_face.shape)
    gathered = lax.all_to_all(copies, "circ", 0, 0, tiled=True)
    row_iota = jnp.arange(rows_local, dtype=jnp.int32)
    first_row = lax.axis_index("circ") * rows_local
    source_rows = (first_row + row_iota[:, None] - offsets[None, :]) % total_rows
    global_rows = jnp.arange(total_rows, dtype=jnp.int32).reshape(circ_count, rows_local)
    picks = global_rows[:, None, :, None, None] == source_rows[None, None, None]
    rotated = jnp.sum(
        jnp.where(picks, gathered[:, :, :, None, :], 0.0), axis=(0, 2)
    )
    panels = rotated.reshape(NF, rows_local, KP_DEV, PW)
    table_ids = jnp.arange(weight_table.shape[0], dtype=jnp.int32)
    weights = jnp.sum(jnp.where(weight_idx[..., None] == table_ids, weight_table, 0.0), axis=-1)
    owner_of = owners[0].reshape(-1)
    slot_of = slots[0].reshape(-1)
    weight_of = weights[0].reshape(-1)
    entries = owner_of.shape[0]
    panel_of = jnp.arange(entries, dtype=jnp.int32) // owners.shape[-1]
    earlier = jnp.tril(jnp.ones((entries, entries), dtype=bool), -1)
    position = jnp.sum(earlier & (owner_of[:, None] == owner_of[None, :]), axis=1)
    chosen = (owner_of[None, None] == jnp.arange(span_count, dtype=jnp.int32)[:, None, None]) & (
        position[None, None] == jnp.arange(CAP, dtype=jnp.int32)[None, :, None]
    )
    picked = jnp.where(chosen, weight_of, 0.0)
    selection = jnp.sum(
        picked[..., None] * (panel_of[:, None] == jnp.arange(KP_DEV, dtype=jnp.int32)), axis=2
    )
    data = jnp.einsum("opk,ftkq->opftq", selection, panels, precision=lax.Precision.HIGHEST)
    code = jnp.sum(jnp.where(chosen, slot_of + 1, 0), axis=2).astype(jnp.float32) - 1.0
    payload = jnp.concatenate(
        [data.reshape(span_count, CAP, -1), code[..., None]], axis=-1
    )
    received = lax.all_to_all(payload, "span", 0, 0, tiled=True)
    values = received[..., :-1].reshape(span_count * CAP, NF, rows_local, 1, PW)
    codes = received[..., -1].reshape(span_count * CAP, 1, 1, 1, 1)
    slot_ids = jnp.arange(KP_DEV, dtype=jnp.float32).reshape(1, 1, 1, KP_DEV, 1)
    inlet_rows = jnp.transpose(
        jnp.sum(jnp.where(codes == slot_ids, values, 0.0), axis=0), (1, 0, 2, 3)
    ).reshape(rows_local, NF, KP_DEV * PW)

    mid, mid_edges = sweep(q_old, q_old, pseudo_rate, inlet_rows, flux_jacobians)
    mid_parts = halo_parts(mid, mid_edges)
    new, _ = sweep(mid, q_old, pseudo_rate, inlet_rows, flux_jacobians, mid_parts)
    return new


def solution(mesh):
    return jax.shard_map(
        body,
        mesh=mesh,
        in_specs=(
            P(None, "circ", "span", None),
            P("circ", "span", None),
            P(),
            P(None, "circ", "span"),
            P("span"),
            P("circ", "span", None),
            P("circ", "span", None),
            P("circ", "span", None),
            P(),
        ),
        out_specs=P(None, "circ", "span", None),
        check_vma=False,
    )
```

```python
import jax
import jax.numpy as jnp
from jax import lax
from jax.experimental import pallas as pl
from jax.experimental.pallas import tpu as pltpu
from jax.sharding import PartitionSpec as P

NF = 5
KP_DEV = 4
PW = 32
CAP = 2


inv_step = 0.5
viscosity = 0.1


def with_halo(block, sides, width):
    for axis, dim in sides:
        count = lax.axis_size(axis)
        forward = [(i, i + 1) for i in range(count - 1)]
        forward.append((count - 1, 0))
        backward = [(target, source) for source, target in forward]
        low = lax.ppermute(
            lax.slice_in_dim(block, block.shape[dim] - width, None, axis=dim), axis, forward
        )
        high = lax.ppermute(lax.slice_in_dim(block, 0, width, axis=dim), axis, backward)
        block = jnp.concatenate([low, block, high], axis=dim)
    return block


def halo_parts(block, span_edges=None):
    parts = []
    for axis, dim in (("circ", 1), ("span", 2)):
        if dim == 2 and span_edges is not None:
            count = lax.axis_size(axis)
            forward = [(i, (i + 1) % count) for i in range(count)]
            backward = [(target, source) for source, target in forward]
            parts += [
                lax.ppermute(span_edges[1], axis, forward),
                lax.ppermute(span_edges[0], axis, backward),
            ]
            continue
        count = lax.axis_size(axis)
        forward = [(i, (i + 1) % count) for i in range(count)]
        backward = [(target, source) for source, target in forward]
        low = lax.ppermute(lax.slice_in_dim(block, block.shape[dim] - 1, None, axis=dim), axis, forward)
        high = lax.ppermute(lax.slice_in_dim(block, 0, 1, axis=dim), axis, backward)
        parts += [low, high]
    span_index = lax.axis_index("span")
    span_last = lax.axis_size("span") - 1
    parts[2] = parts[2] * (span_index != 0).astype(block.dtype)
    parts[3] = parts[3] * (span_index != span_last).astype(block.dtype)
    return parts


def lateral_of(block, parts):
    circ_low, circ_high, span_low, span_high = parts
    return (
        jnp.concatenate([block[:, 1:], circ_high], axis=1),
        jnp.concatenate([circ_low, block[:, :-1]], axis=1),
        jnp.concatenate([block[:, :, 1:], span_high], axis=2),
        jnp.concatenate([span_low, block[:, :, :-1]], axis=2),
    )


def stencil_kernel(
    j_ref, c_ref, cu_ref, cd_ref, su_ref, sd_ref, prev_ref, rate_ref, inlet_ref,
    out_ref, first_ref, last_ref, inlet_scr,
):
    span, axial = inlet_scr.shape[1:]
    for g in range(NF):
        row = inlet_ref[0, g : g + 1, :]
        inlet_scr[g] = jnp.transpose(jnp.broadcast_to(row, (axial, span)))
    lane = lax.broadcasted_iota(jnp.int32, (8, 128), 1)
    probe = pltpu.roll(lane, 1, 1)
    numpy_order = probe == (lane + 127) % 128

    def chunk(i, carry):
        rows = pl.ds(pl.multiple_of(i * 8, 8), 8)
        cur = [c_ref[g, 0, rows, :] for g in range(NF)]
        cu = [cu_ref[g, 0, rows, :] for g in range(NF)]
        cd = [cd_ref[g, 0, rows, :] for g in range(NF)]
        su = [su_ref[g, 0, rows, :] for g in range(NF)]
        sd = [sd_ref[g, 0, rows, :] for g in range(NF)]
        au, ad = [], []
        for g in range(NF):
            one = pltpu.roll(cur[g], 1, 1)
            other = pltpu.roll(cur[g], 127, 1)
            down = jnp.where(numpy_order, one, other)
            up = jnp.where(numpy_order, other, one)
            ad.append(jnp.where(lane == 0, inlet_scr[g, rows, :], down))
            au.append(jnp.where(lane == 127, 0.0, up))
        dc = [cu[g] - cd[g] for g in range(NF)]
        ds = [su[g] - sd[g] for g in range(NF)]
        da = [au[g] - ad[g] for g in range(NF)]
        rate = rate_ref[0, rows, :]
        for f in range(NF):
            convection = None
            for d, diff in enumerate((dc, ds, da)):
                term = j_ref[d * NF * NF + f * NF] * diff[0]
                for g in range(1, NF):
                    term = term + j_ref[d * NF * NF + f * NF + g] * diff[g]
                convection = term if convection is None else convection + term
            laplacian = cu[f] + cd[f] + (su[f] + sd[f]) + (au[f] + ad[f]) - 6.0 * cur[f]
            residual = (
                inv_step * (cur[f] - prev_ref[f, 0, rows, :])
                + 0.5 * convection
                - viscosity * laplacian
            )
            out_ref[f, 0, rows, :] = cur[f] - rate * residual
        return carry

    lax.fori_loop(0, c_ref.shape[2] // 8, chunk, 0)
    first_ref[...] = out_ref[:, :, 0:1, :]
    last_ref[...] = out_ref[:, :, span - 1 : span, :]


def sweep(current, previous, rate_cells, inlet_rows, jacobians, parts=None):
    if parts is None:
        parts = halo_parts(current)
    circ_low, circ_high, span_low, span_high = parts
    padded = jnp.concatenate([circ_low, current, circ_high], axis=1)
    span_up = jnp.concatenate([current[:, :, 1:], span_high], axis=2)
    span_down = jnp.concatenate([span_low, current[:, :, :-1]], axis=2)
    nf, rows, span, axial = current.shape
    block = (nf, 1, span, axial)
    spec = lambda shift: pl.BlockSpec(block, lambda t: (0, t + shift, 0, 0))
    out = pl.pallas_call(
        stencil_kernel,
        grid=(rows,),
        in_specs=[
            pl.BlockSpec(memory_space=pltpu.SMEM),
            spec(1),
            spec(2),
            spec(0),
            spec(0),
            spec(0),
            spec(0),
            pl.BlockSpec((1, span, axial), lambda t: (t, 0, 0)),
            pl.BlockSpec((1, nf, span), lambda t: (t, 0, 0)),
        ],
        scratch_shapes=[pltpu.VMEM((nf, span, axial), current.dtype)],
        out_specs=[spec(0)] + [pl.BlockSpec((nf, 1, 1, axial), lambda t: (0, t, 0, 0))] * 2,
        out_shape=[jax.ShapeDtypeStruct(current.shape, current.dtype)]
        + [jax.ShapeDtypeStruct((nf, rows, 1, axial), current.dtype)] * 2,
    )(jacobians.reshape(-1), padded, padded, padded, span_up, span_down, previous, rate_cells, inlet_rows)
    out, first, last = out
    return out, (first, last)


def contract(matrix, values):
    column = lambda g: matrix[:, g].reshape((-1,) + (1,) * (values.ndim - 1))
    total = column(0) * values[0][None]
    for g in range(1, matrix.shape[1]):
        total = total + column(g) * values[g][None]
    return total


def update(current, previous, rate_cells, neighbours, jacobians):
    circ_up, circ_down, span_up, span_down, axial_up, axial_down = neighbours
    convection = contract(jacobians[0], circ_up - circ_down)
    convection = convection + contract(jacobians[1], span_up - span_down)
    convection = convection + contract(jacobians[2], axial_up - axial_down)
    laplacian = (
        circ_up + circ_down + (span_up + span_down) + (axial_up + axial_down) - 6.0 * current
    )
    residual = inv_step * (current - previous) + 0.5 * convection - viscosity * laplacian
    return current - rate_cells[None] * residual


def lateral(padded):
    return (
        padded[:, 2:, 1:-1],
        padded[:, :-2, 1:-1],
        padded[:, 1:-1, 2:],
        padded[:, 1:-1, :-2],
    )


def advance(padded, current, previous, rate_cells, jacobians):
    zero_column = jnp.zeros_like(current[..., :1])
    axial_up = jnp.concatenate([current[..., 1:], zero_column], axis=-1)
    axial_down = jnp.concatenate([zero_column, current[..., :-1]], axis=-1)
    neighbours = lateral(padded) + (axial_up, axial_down)
    return update(current, previous, rate_cells, neighbours, jacobians)


def wall_zero(field_array, width):
    span_index = lax.axis_index("span")
    span_count = lax.axis_size("span")
    length = field_array.shape[2]
    position = jnp.arange(length, dtype=jnp.int32)
    at_hub = jnp.logical_and(span_index == 0, position < width)
    at_tip = jnp.logical_and(span_index == span_count - 1, position >= length - width)
    keeping = jnp.logical_not(jnp.logical_or(at_hub, at_tip)).astype(field_array.dtype)
    keeping = keeping.reshape(1, 1, length, 1)
    return field_array * keeping


def body(
    q_old, pseudo_rate, flux_jacobians, rotor_face, offsets, owners, slots, weight_idx, weight_table
):
    circ_count = lax.axis_size("circ")
    span_count = lax.axis_size("span")
    rows_local = rotor_face.shape[1]
    total_rows = rows_local * circ_count
    copies = jnp.broadcast_to(rotor_face[None], (circ_count,) + rotor_face.shape)
    gathered = lax.all_to_all(copies, "circ", 0, 0, tiled=True)
    row_iota = jnp.arange(rows_local, dtype=jnp.int32)
    first_row = lax.axis_index("circ") * rows_local
    source_rows = (first_row + row_iota[:, None] - offsets[None, :]) % total_rows
    global_rows = jnp.arange(total_rows, dtype=jnp.int32).reshape(circ_count, rows_local)
    picks = global_rows[:, None, :, None, None] == source_rows[None, None, None]
    rotated = jnp.sum(
        jnp.where(picks, gathered[:, :, :, None, :], 0.0), axis=(0, 2)
    )
    panels = rotated.reshape(NF, rows_local, KP_DEV, PW)
    table_ids = jnp.arange(weight_table.shape[0], dtype=jnp.int32)
    weights = jnp.sum(jnp.where(weight_idx[..., None] == table_ids, weight_table, 0.0), axis=-1)
    owner_of = owners[0].reshape(-1)
    slot_of = slots[0].reshape(-1)
    weight_of = weights[0].reshape(-1)
    entries = owner_of.shape[0]
    panel_of = jnp.arange(entries, dtype=jnp.int32) // owners.shape[-1]
    earlier = jnp.tril(jnp.ones((entries, entries), dtype=bool), -1)
    position = jnp.sum(earlier & (owner_of[:, None] == owner_of[None, :]), axis=1)
    chosen = (owner_of[None, None] == jnp.arange(span_count, dtype=jnp.int32)[:, None, None]) & (
        position[None, None] == jnp.arange(CAP, dtype=jnp.int32)[None, :, None]
    )
    picked = jnp.where(chosen, weight_of, 0.0)
    selection = jnp.sum(
        picked[..., None] * (panel_of[:, None] == jnp.arange(KP_DEV, dtype=jnp.int32)), axis=2
    )
    data = jnp.einsum("opk,ftkq->opftq", selection, panels, precision=lax.Precision.HIGHEST)
    code = jnp.sum(jnp.where(chosen, slot_of + 1, 0), axis=2).astype(jnp.float32) - 1.0
    payload = jnp.concatenate(
        [data.reshape(span_count, CAP, -1), code[..., None]], axis=-1
    )
    received = lax.all_to_all(payload, "span", 0, 0, tiled=True)
    values = received[..., :-1].reshape(span_count * CAP, NF, rows_local, 1, PW)
    codes = received[..., -1].reshape(span_count * CAP, 1, 1, 1, 1)
    slot_ids = jnp.arange(KP_DEV, dtype=jnp.float32).reshape(1, 1, 1, KP_DEV, 1)
    inlet_rows = jnp.transpose(
        jnp.sum(jnp.where(codes == slot_ids, values, 0.0), axis=0), (1, 0, 2, 3)
    ).reshape(rows_local, NF, KP_DEV * PW)

    mid, mid_edges = sweep(q_old, q_old, pseudo_rate, inlet_rows, flux_jacobians)
    mid_parts = halo_parts(mid, mid_edges)
    new, _ = sweep(mid, q_old, pseudo_rate, inlet_rows, flux_jacobians, mid_parts)
    return new


def solution(mesh):
    return jax.shard_map(
        body,
        mesh=mesh,
        in_specs=(
            P(None, "circ", "span", None),
            P("circ", "span", None),
            P(),
            P(None, "circ", "span"),
            P("span"),
            P("circ", "span", None),
            P("circ", "span", None),
            P("circ", "span", None),
            P(),
        ),
        out_specs=P(None, "circ", "span", None),
        check_vma=False,
    )
```

```python
import jax
import jax.numpy as jnp
from jax import lax
from jax.experimental import pallas as pl
from jax.experimental.pallas import tpu as pltpu
from jax.sharding import PartitionSpec as P

NF = 5
KP_DEV = 4
PW = 32
CAP = 2


inv_step = 0.5
viscosity = 0.1


def with_halo(block, sides, width):
    for axis, dim in sides:
        count = lax.axis_size(axis)
        forward = [(i, i + 1) for i in range(count - 1)]
        forward.append((count - 1, 0))
        backward = [(target, source) for source, target in forward]
        low = lax.ppermute(
            lax.slice_in_dim(block, block.shape[dim] - width, None, axis=dim), axis, forward
        )
        high = lax.ppermute(lax.slice_in_dim(block, 0, width, axis=dim), axis, backward)
        block = jnp.concatenate([low, block, high], axis=dim)
    return block


def halo_parts(block, edges=None):
    parts = []
    for axis, dim in (("circ", 1), ("span", 2)):
        if edges is not None:
            count = lax.axis_size(axis)
            forward = [(i, (i + 1) % count) for i in range(count)]
            backward = [(target, source) for source, target in forward]
            first, last = edges[2:] if dim == 1 else edges[:2]
            parts += [lax.ppermute(last, axis, forward), lax.ppermute(first, axis, backward)]
            continue
        count = lax.axis_size(axis)
        forward = [(i, (i + 1) % count) for i in range(count)]
        backward = [(target, source) for source, target in forward]
        low = lax.ppermute(lax.slice_in_dim(block, block.shape[dim] - 1, None, axis=dim), axis, forward)
        high = lax.ppermute(lax.slice_in_dim(block, 0, 1, axis=dim), axis, backward)
        parts += [low, high]
    span_index = lax.axis_index("span")
    span_last = lax.axis_size("span") - 1
    parts[2] = parts[2] * (span_index != 0).astype(block.dtype)
    parts[3] = parts[3] * (span_index != span_last).astype(block.dtype)
    return parts


def lateral_of(block, parts):
    circ_low, circ_high, span_low, span_high = parts
    return (
        jnp.concatenate([block[:, 1:], circ_high], axis=1),
        jnp.concatenate([circ_low, block[:, :-1]], axis=1),
        jnp.concatenate([block[:, :, 1:], span_high], axis=2),
        jnp.concatenate([span_low, block[:, :, :-1]], axis=2),
    )


def stencil_kernel(
    j_ref, c_ref, cu_ref, cd_ref, su_ref, sd_ref, prev_ref, rate_ref, inlet_ref,
    out_ref, first_ref, last_ref, top_ref, bottom_ref, inlet_scr,
):
    span, axial = inlet_scr.shape[1:]
    for g in range(NF):
        row = inlet_ref[0, g : g + 1, :]
        inlet_scr[g] = jnp.transpose(jnp.broadcast_to(row, (axial, span)))
    lane = lax.broadcasted_iota(jnp.int32, (8, 128), 1)
    probe = pltpu.roll(lane, 1, 1)
    numpy_order = probe == (lane + 127) % 128

    def chunk(i, carry):
        rows = pl.ds(pl.multiple_of(i * 8, 8), 8)
        cur = [c_ref[g, 0, rows, :] for g in range(NF)]
        cu = [cu_ref[g, 0, rows, :] for g in range(NF)]
        cd = [cd_ref[g, 0, rows, :] for g in range(NF)]
        su = [su_ref[g, 0, rows, :] for g in range(NF)]
        sd = [sd_ref[g, 0, rows, :] for g in range(NF)]
        au, ad = [], []
        for g in range(NF):
            one = pltpu.roll(cur[g], 1, 1)
            other = pltpu.roll(cur[g], 127, 1)
            down = jnp.where(numpy_order, one, other)
            up = jnp.where(numpy_order, other, one)
            ad.append(jnp.where(lane == 0, inlet_scr[g, rows, :], down))
            au.append(jnp.where(lane == 127, 0.0, up))
        dc = [cu[g] - cd[g] for g in range(NF)]
        ds = [su[g] - sd[g] for g in range(NF)]
        da = [au[g] - ad[g] for g in range(NF)]
        rate = rate_ref[0, rows, :]
        for f in range(NF):
            convection = None
            for d, diff in enumerate((dc, ds, da)):
                term = j_ref[d * NF * NF + f * NF] * diff[0]
                for g in range(1, NF):
                    term = term + j_ref[d * NF * NF + f * NF + g] * diff[g]
                convection = term if convection is None else convection + term
            laplacian = cu[f] + cd[f] + (su[f] + sd[f]) + (au[f] + ad[f]) - 6.0 * cur[f]
            residual = (
                inv_step * (cur[f] - prev_ref[f, 0, rows, :])
                + 0.5 * convection
                - viscosity * laplacian
            )
            out_ref[f, 0, rows, :] = cur[f] - rate * residual
        return carry

    lax.fori_loop(0, c_ref.shape[2] // 8, chunk, 0)
    first_ref[...] = out_ref[:, :, 0:1, :]
    last_ref[...] = out_ref[:, :, span - 1 : span, :]

    @pl.when(pl.program_id(0) == 0)
    def _():
        top_ref[...] = out_ref[...]

    @pl.when(pl.program_id(0) == pl.num_programs(0) - 1)
    def _():
        bottom_ref[...] = out_ref[...]


def sweep(current, previous, rate_cells, inlet_rows, jacobians, parts=None):
    if parts is None:
        parts = halo_parts(current)
    circ_low, circ_high, span_low, span_high = parts
    padded = jnp.concatenate([circ_low, current, circ_high], axis=1)
    span_up = jnp.concatenate([current[:, :, 1:], span_high], axis=2)
    span_down = jnp.concatenate([span_low, current[:, :, :-1]], axis=2)
    nf, rows, span, axial = current.shape
    block = (nf, 1, span, axial)
    spec = lambda shift: pl.BlockSpec(block, lambda t: (0, t + shift, 0, 0))
    out = pl.pallas_call(
        stencil_kernel,
        grid=(rows,),
        in_specs=[
            pl.BlockSpec(memory_space=pltpu.SMEM),
            spec(1),
            spec(2),
            spec(0),
            spec(0),
            spec(0),
            spec(0),
            pl.BlockSpec((1, span, axial), lambda t: (t, 0, 0)),
            pl.BlockSpec((1, nf, span), lambda t: (t, 0, 0)),
        ],
        scratch_shapes=[pltpu.VMEM((nf, span, axial), current.dtype)],
        out_specs=[spec(0)]
        + [pl.BlockSpec((nf, 1, 1, axial), lambda t: (0, t, 0, 0))] * 2
        + [pl.BlockSpec(block, lambda t: (0, 0, 0, 0))] * 2,
        out_shape=[jax.ShapeDtypeStruct(current.shape, current.dtype)]
        + [jax.ShapeDtypeStruct((nf, rows, 1, axial), current.dtype)] * 2
        + [jax.ShapeDtypeStruct(block, current.dtype)] * 2,
    )(jacobians.reshape(-1), padded, padded, padded, span_up, span_down, previous, rate_cells, inlet_rows)
    out, first, last, top, bottom = out
    return out, (first, last, top, bottom)


def contract(matrix, values):
    column = lambda g: matrix[:, g].reshape((-1,) + (1,) * (values.ndim - 1))
    total = column(0) * values[0][None]
    for g in range(1, matrix.shape[1]):
        total = total + column(g) * values[g][None]
    return total


def update(current, previous, rate_cells, neighbours, jacobians):
    circ_up, circ_down, span_up, span_down, axial_up, axial_down = neighbours
    convection = contract(jacobians[0], circ_up - circ_down)
    convection = convection + contract(jacobians[1], span_up - span_down)
    convection = convection + contract(jacobians[2], axial_up - axial_down)
    laplacian = (
        circ_up + circ_down + (span_up + span_down) + (axial_up + axial_down) - 6.0 * current
    )
    residual = inv_step * (current - previous) + 0.5 * convection - viscosity * laplacian
    return current - rate_cells[None] * residual


def lateral(padded):
    return (
        padded[:, 2:, 1:-1],
        padded[:, :-2, 1:-1],
        padded[:, 1:-1, 2:],
        padded[:, 1:-1, :-2],
    )


def advance(padded, current, previous, rate_cells, jacobians):
    zero_column = jnp.zeros_like(current[..., :1])
    axial_up = jnp.concatenate([current[..., 1:], zero_column], axis=-1)
    axial_down = jnp.concatenate([zero_column, current[..., :-1]], axis=-1)
    neighbours = lateral(padded) + (axial_up, axial_down)
    return update(current, previous, rate_cells, neighbours, jacobians)


def wall_zero(field_array, width):
    span_index = lax.axis_index("span")
    span_count = lax.axis_size("span")
    length = field_array.shape[2]
    position = jnp.arange(length, dtype=jnp.int32)
    at_hub = jnp.logical_and(span_index == 0, position < width)
    at_tip = jnp.logical_and(span_index == span_count - 1, position >= length - width)
    keeping = jnp.logical_not(jnp.logical_or(at_hub, at_tip)).astype(field_array.dtype)
    keeping = keeping.reshape(1, 1, length, 1)
    return field_array * keeping


def body(
    q_old, pseudo_rate, flux_jacobians, rotor_face, offsets, owners, slots, weight_idx, weight_table
):
    circ_count = lax.axis_size("circ")
    span_count = lax.axis_size("span")
    rows_local = rotor_face.shape[1]
    total_rows = rows_local * circ_count
    copies = jnp.broadcast_to(rotor_face[None], (circ_count,) + rotor_face.shape)
    gathered = lax.all_to_all(copies, "circ", 0, 0, tiled=True)
    row_iota = jnp.arange(rows_local, dtype=jnp.int32)
    first_row = lax.axis_index("circ") * rows_local
    source_rows = (first_row + row_iota[:, None] - offsets[None, :]) % total_rows
    global_rows = jnp.arange(total_rows, dtype=jnp.int32).reshape(circ_count, rows_local)
    picks = global_rows[:, None, :, None, None] == source_rows[None, None, None]
    rotated = jnp.sum(
        jnp.where(picks, gathered[:, :, :, None, :], 0.0), axis=(0, 2)
    )
    panels = rotated.reshape(NF, rows_local, KP_DEV, PW)
    table_ids = jnp.arange(weight_table.shape[0], dtype=jnp.int32)
    weights = jnp.sum(jnp.where(weight_idx[..., None] == table_ids, weight_table, 0.0), axis=-1)
    owner_of = owners[0].reshape(-1)
    slot_of = slots[0].reshape(-1)
    weight_of = weights[0].reshape(-1)
    entries = owner_of.shape[0]
    panel_of = jnp.arange(entries, dtype=jnp.int32) // owners.shape[-1]
    earlier = jnp.tril(jnp.ones((entries, entries), dtype=bool), -1)
    position = jnp.sum(earlier & (owner_of[:, None] == owner_of[None, :]), axis=1)
    chosen = (owner_of[None, None] == jnp.arange(span_count, dtype=jnp.int32)[:, None, None]) & (
        position[None, None] == jnp.arange(CAP, dtype=jnp.int32)[None, :, None]
    )
    picked = jnp.where(chosen, weight_of, 0.0)
    selection = jnp.sum(
        picked[..., None] * (panel_of[:, None] == jnp.arange(KP_DEV, dtype=jnp.int32)), axis=2
    )
    data = jnp.einsum("opk,ftkq->opftq", selection, panels, precision=lax.Precision.HIGHEST)
    code = jnp.sum(jnp.where(chosen, slot_of + 1, 0), axis=2).astype(jnp.float32) - 1.0
    payload = jnp.concatenate(
        [data.reshape(span_count, CAP, -1), code[..., None]], axis=-1
    )
    received = lax.all_to_all(payload, "span", 0, 0, tiled=True)
    values = received[..., :-1].reshape(span_count * CAP, NF, rows_local, 1, PW)
    codes = received[..., -1].reshape(span_count * CAP, 1, 1, 1, 1)
    slot_ids = jnp.arange(KP_DEV, dtype=jnp.float32).reshape(1, 1, 1, KP_DEV, 1)
    inlet_rows = jnp.transpose(
        jnp.sum(jnp.where(codes == slot_ids, values, 0.0), axis=0), (1, 0, 2, 3)
    ).reshape(rows_local, NF, KP_DEV * PW)

    mid, mid_edges = sweep(q_old, q_old, pseudo_rate, inlet_rows, flux_jacobians)
    mid_parts = halo_parts(mid, mid_edges)
    new, _ = sweep(mid, q_old, pseudo_rate, inlet_rows, flux_jacobians, mid_parts)
    return new


def solution(mesh):
    return jax.shard_map(
        body,
        mesh=mesh,
        in_specs=(
            P(None, "circ", "span", None),
            P("circ", "span", None),
            P(),
            P(None, "circ", "span"),
            P("span"),
            P("circ", "span", None),
            P("circ", "span", None),
            P("circ", "span", None),
            P(),
        ),
        out_specs=P(None, "circ", "span", None),
        check_vma=False,
    )
```

```python
import jax
import jax.numpy as jnp
from jax import lax
from jax.experimental import pallas as pl
from jax.experimental.pallas import tpu as pltpu
from jax.sharding import PartitionSpec as P

NF = 5
KP_DEV = 4
PW = 32
CAP = 2


inv_step = 0.5
viscosity = 0.1


def with_halo(block, sides, width):
    for axis, dim in sides:
        count = lax.axis_size(axis)
        forward = [(i, i + 1) for i in range(count - 1)]
        forward.append((count - 1, 0))
        backward = [(target, source) for source, target in forward]
        low = lax.ppermute(
            lax.slice_in_dim(block, block.shape[dim] - width, None, axis=dim), axis, forward
        )
        high = lax.ppermute(lax.slice_in_dim(block, 0, width, axis=dim), axis, backward)
        block = jnp.concatenate([low, block, high], axis=dim)
    return block


def halo_parts(block, edges=None):
    parts = []
    for axis, dim in (("circ", 1), ("span", 2)):
        if edges is not None:
            count = lax.axis_size(axis)
            forward = [(i, (i + 1) % count) for i in range(count)]
            backward = [(target, source) for source, target in forward]
            first, last = edges[2:] if dim == 1 else edges[:2]
            parts += [lax.ppermute(last, axis, forward), lax.ppermute(first, axis, backward)]
            continue
        count = lax.axis_size(axis)
        forward = [(i, (i + 1) % count) for i in range(count)]
        backward = [(target, source) for source, target in forward]
        low = lax.ppermute(lax.slice_in_dim(block, block.shape[dim] - 1, None, axis=dim), axis, forward)
        high = lax.ppermute(lax.slice_in_dim(block, 0, 1, axis=dim), axis, backward)
        parts += [low, high]
    span_index = lax.axis_index("span")
    span_last = lax.axis_size("span") - 1
    parts[2] = parts[2] * (span_index != 0).astype(block.dtype)
    parts[3] = parts[3] * (span_index != span_last).astype(block.dtype)
    return parts


def lateral_of(block, parts):
    circ_low, circ_high, span_low, span_high = parts
    return (
        jnp.concatenate([block[:, 1:], circ_high], axis=1),
        jnp.concatenate([circ_low, block[:, :-1]], axis=1),
        jnp.concatenate([block[:, :, 1:], span_high], axis=2),
        jnp.concatenate([span_low, block[:, :, :-1]], axis=2),
    )


def stencil_kernel(
    j_ref, c_ref, cu_ref, cd_ref, su_ref, sd_ref, prev_ref, rate_ref, inlet_ref,
    out_ref, first_ref, last_ref, top_ref, bottom_ref, inlet_scr,
):
    span, axial = inlet_scr.shape[1:]
    for g in range(NF):
        row = inlet_ref[0, g : g + 1, :]
        inlet_scr[g] = jnp.transpose(jnp.broadcast_to(row, (axial, span)))
    lane = lax.broadcasted_iota(jnp.int32, (8, 128), 1)
    probe = pltpu.roll(lane, 1, 1)
    numpy_order = probe == (lane + 127) % 128

    def chunk(i, carry):
        rows = pl.ds(pl.multiple_of(i * 8, 8), 8)
        cur = [c_ref[g, 0, rows, :] for g in range(NF)]
        cu = [cu_ref[g, 0, rows, :] for g in range(NF)]
        cd = [cd_ref[g, 0, rows, :] for g in range(NF)]
        su = [su_ref[g, 0, rows, :] for g in range(NF)]
        sd = [sd_ref[g, 0, rows, :] for g in range(NF)]
        au, ad = [], []
        for g in range(NF):
            one = pltpu.roll(cur[g], 1, 1)
            other = pltpu.roll(cur[g], 127, 1)
            down = jnp.where(numpy_order, one, other)
            up = jnp.where(numpy_order, other, one)
            ad.append(jnp.where(lane == 0, inlet_scr[g, rows, :], down))
            au.append(jnp.where(lane == 127, 0.0, up))
        dc = [cu[g] - cd[g] for g in range(NF)]
        ds = [su[g] - sd[g] for g in range(NF)]
        da = [au[g] - ad[g] for g in range(NF)]
        rate = rate_ref[0, rows, :]
        for f in range(NF):
            convection = None
            for d, diff in enumerate((dc, ds, da)):
                term = j_ref[d * NF * NF + f * NF] * diff[0]
                for g in range(1, NF):
                    term = term + j_ref[d * NF * NF + f * NF + g] * diff[g]
                convection = term if convection is None else convection + term
            laplacian = cu[f] + cd[f] + (su[f] + sd[f]) + (au[f] + ad[f]) - 6.0 * cur[f]
            residual = (
                inv_step * (cur[f] - prev_ref[f, 0, rows, :])
                + 0.5 * convection
                - viscosity * laplacian
            )
            out_ref[f, 0, rows, :] = cur[f] - rate * residual
        return carry

    lax.fori_loop(0, c_ref.shape[2] // 8, chunk, 0)
    first_ref[...] = out_ref[:, :, 0:1, :]
    last_ref[...] = out_ref[:, :, span - 1 : span, :]

    @pl.when(pl.program_id(0) == 0)
    def _():
        top_ref[...] = out_ref[...]

    @pl.when(pl.program_id(0) == pl.num_programs(0) - 1)
    def _():
        bottom_ref[...] = out_ref[...]


def sweep(current, previous, rate_cells, inlet_rows, jacobians, parts=None):
    if parts is None:
        parts = halo_parts(current)
    circ_low, circ_high, span_low, span_high = parts
    padded = jnp.concatenate([circ_low, current, circ_high], axis=1)
    span_row = lax.broadcasted_iota(jnp.int32, current.shape, 2)
    span_up = jnp.where(span_row == current.shape[2] - 1, span_high, jnp.roll(current, -1, axis=2))
    span_down = jnp.where(span_row == 0, span_low, jnp.roll(current, 1, axis=2))
    nf, rows, span, axial = current.shape
    block = (nf, 1, span, axial)
    spec = lambda shift: pl.BlockSpec(block, lambda t: (0, t + shift, 0, 0))
    out = pl.pallas_call(
        stencil_kernel,
        grid=(rows,),
        in_specs=[
            pl.BlockSpec(memory_space=pltpu.SMEM),
            spec(1),
            spec(2),
            spec(0),
            spec(0),
            spec(0),
            spec(0),
            pl.BlockSpec((1, span, axial), lambda t: (t, 0, 0)),
            pl.BlockSpec((1, nf, span), lambda t: (t, 0, 0)),
        ],
        scratch_shapes=[pltpu.VMEM((nf, span, axial), current.dtype)],
        out_specs=[spec(0)]
        + [pl.BlockSpec((nf, 1, 1, axial), lambda t: (0, t, 0, 0))] * 2
        + [pl.BlockSpec(block, lambda t: (0, 0, 0, 0))] * 2,
        out_shape=[jax.ShapeDtypeStruct(current.shape, current.dtype)]
        + [jax.ShapeDtypeStruct((nf, rows, 1, axial), current.dtype)] * 2
        + [jax.ShapeDtypeStruct(block, current.dtype)] * 2,
    )(jacobians.reshape(-1), padded, padded, padded, span_up, span_down, previous, rate_cells, inlet_rows)
    out, first, last, top, bottom = out
    return out, (first, last, top, bottom)


def contract(matrix, values):
    column = lambda g: matrix[:, g].reshape((-1,) + (1,) * (values.ndim - 1))
    total = column(0) * values[0][None]
    for g in range(1, matrix.shape[1]):
        total = total + column(g) * values[g][None]
    return total


def update(current, previous, rate_cells, neighbours, jacobians):
    circ_up, circ_down, span_up, span_down, axial_up, axial_down = neighbours
    convection = contract(jacobians[0], circ_up - circ_down)
    convection = convection + contract(jacobians[1], span_up - span_down)
    convection = convection + contract(jacobians[2], axial_up - axial_down)
    laplacian = (
        circ_up + circ_down + (span_up + span_down) + (axial_up + axial_down) - 6.0 * current
    )
    residual = inv_step * (current - previous) + 0.5 * convection - viscosity * laplacian
    return current - rate_cells[None] * residual


def lateral(padded):
    return (
        padded[:, 2:, 1:-1],
        padded[:, :-2, 1:-1],
        padded[:, 1:-1, 2:],
        padded[:, 1:-1, :-2],
    )


def advance(padded, current, previous, rate_cells, jacobians):
    zero_column = jnp.zeros_like(current[..., :1])
    axial_up = jnp.concatenate([current[..., 1:], zero_column], axis=-1)
    axial_down = jnp.concatenate([zero_column, current[..., :-1]], axis=-1)
    neighbours = lateral(padded) + (axial_up, axial_down)
    return update(current, previous, rate_cells, neighbours, jacobians)


def wall_zero(field_array, width):
    span_index = lax.axis_index("span")
    span_count = lax.axis_size("span")
    length = field_array.shape[2]
    position = jnp.arange(length, dtype=jnp.int32)
    at_hub = jnp.logical_and(span_index == 0, position < width)
    at_tip = jnp.logical_and(span_index == span_count - 1, position >= length - width)
    keeping = jnp.logical_not(jnp.logical_or(at_hub, at_tip)).astype(field_array.dtype)
    keeping = keeping.reshape(1, 1, length, 1)
    return field_array * keeping


def body(
    q_old, pseudo_rate, flux_jacobians, rotor_face, offsets, owners, slots, weight_idx, weight_table
):
    circ_count = lax.axis_size("circ")
    span_count = lax.axis_size("span")
    rows_local = rotor_face.shape[1]
    total_rows = rows_local * circ_count
    copies = jnp.broadcast_to(rotor_face[None], (circ_count,) + rotor_face.shape)
    gathered = lax.all_to_all(copies, "circ", 0, 0, tiled=True)
    row_iota = jnp.arange(rows_local, dtype=jnp.int32)
    first_row = lax.axis_index("circ") * rows_local
    source_rows = (first_row + row_iota[:, None] - offsets[None, :]) % total_rows
    global_rows = jnp.arange(total_rows, dtype=jnp.int32).reshape(circ_count, rows_local)
    picks = global_rows[:, None, :, None, None] == source_rows[None, None, None]
    rotated = jnp.sum(
        jnp.where(picks, gathered[:, :, :, None, :], 0.0), axis=(0, 2)
    )
    panels = rotated.reshape(NF, rows_local, KP_DEV, PW)
    table_ids = jnp.arange(weight_table.shape[0], dtype=jnp.int32)
    weights = jnp.sum(jnp.where(weight_idx[..., None] == table_ids, weight_table, 0.0), axis=-1)
    owner_of = owners[0].reshape(-1)
    slot_of = slots[0].reshape(-1)
    weight_of = weights[0].reshape(-1)
    entries = owner_of.shape[0]
    panel_of = jnp.arange(entries, dtype=jnp.int32) // owners.shape[-1]
    earlier = jnp.tril(jnp.ones((entries, entries), dtype=bool), -1)
    position = jnp.sum(earlier & (owner_of[:, None] == owner_of[None, :]), axis=1)
    chosen = (owner_of[None, None] == jnp.arange(span_count, dtype=jnp.int32)[:, None, None]) & (
        position[None, None] == jnp.arange(CAP, dtype=jnp.int32)[None, :, None]
    )
    picked = jnp.where(chosen, weight_of, 0.0)
    selection = jnp.sum(
        picked[..., None] * (panel_of[:, None] == jnp.arange(KP_DEV, dtype=jnp.int32)), axis=2
    )
    data = jnp.einsum("opk,ftkq->opftq", selection, panels, precision=lax.Precision.HIGHEST)
    code = jnp.sum(jnp.where(chosen, slot_of + 1, 0), axis=2).astype(jnp.float32) - 1.0
    payload = jnp.concatenate(
        [data.reshape(span_count, CAP, -1), code[..., None]], axis=-1
    )
    received = lax.all_to_all(payload, "span", 0, 0, tiled=True)
    values = received[..., :-1].reshape(span_count * CAP, NF, rows_local, 1, PW)
    codes = received[..., -1].reshape(span_count * CAP, 1, 1, 1, 1)
    slot_ids = jnp.arange(KP_DEV, dtype=jnp.float32).reshape(1, 1, 1, KP_DEV, 1)
    inlet_rows = jnp.transpose(
        jnp.sum(jnp.where(codes == slot_ids, values, 0.0), axis=0), (1, 0, 2, 3)
    ).reshape(rows_local, NF, KP_DEV * PW)

    mid, mid_edges = sweep(q_old, q_old, pseudo_rate, inlet_rows, flux_jacobians)
    mid_parts = halo_parts(mid, mid_edges)
    new, _ = sweep(mid, q_old, pseudo_rate, inlet_rows, flux_jacobians, mid_parts)
    return new


def solution(mesh):
    return jax.shard_map(
        body,
        mesh=mesh,
        in_specs=(
            P(None, "circ", "span", None),
            P("circ", "span", None),
            P(),
            P(None, "circ", "span"),
            P("span"),
            P("circ", "span", None),
            P("circ", "span", None),
            P("circ", "span", None),
            P(),
        ),
        out_specs=P(None, "circ", "span", None),
        check_vma=False,
    )
```

```python
import jax
import jax.numpy as jnp
from jax import lax
from jax.experimental import pallas as pl
from jax.experimental.pallas import tpu as pltpu
from jax.sharding import PartitionSpec as P

NF = 5
KP_DEV = 4
PW = 32
CAP = 2


inv_step = 0.5
viscosity = 0.1


def with_halo(block, sides, width):
    for axis, dim in sides:
        count = lax.axis_size(axis)
        forward = [(i, i + 1) for i in range(count - 1)]
        forward.append((count - 1, 0))
        backward = [(target, source) for source, target in forward]
        low = lax.ppermute(
            lax.slice_in_dim(block, block.shape[dim] - width, None, axis=dim), axis, forward
        )
        high = lax.ppermute(lax.slice_in_dim(block, 0, width, axis=dim), axis, backward)
        block = jnp.concatenate([low, block, high], axis=dim)
    return block


def halo_parts(block, edges=None):
    parts = []
    for axis, dim in (("circ", 1), ("span", 2)):
        if edges is not None:
            count = lax.axis_size(axis)
            forward = [(i, (i + 1) % count) for i in range(count)]
            backward = [(target, source) for source, target in forward]
            first, last = edges[2:] if dim == 1 else edges[:2]
            parts += [lax.ppermute(last, axis, forward), lax.ppermute(first, axis, backward)]
            continue
        count = lax.axis_size(axis)
        forward = [(i, (i + 1) % count) for i in range(count)]
        backward = [(target, source) for source, target in forward]
        low = lax.ppermute(lax.slice_in_dim(block, block.shape[dim] - 1, None, axis=dim), axis, forward)
        high = lax.ppermute(lax.slice_in_dim(block, 0, 1, axis=dim), axis, backward)
        parts += [low, high]
    span_index = lax.axis_index("span")
    span_last = lax.axis_size("span") - 1
    parts[2] = parts[2] * (span_index != 0).astype(block.dtype)
    parts[3] = parts[3] * (span_index != span_last).astype(block.dtype)
    return parts


def lateral_of(block, parts):
    circ_low, circ_high, span_low, span_high = parts
    return (
        jnp.concatenate([block[:, 1:], circ_high], axis=1),
        jnp.concatenate([circ_low, block[:, :-1]], axis=1),
        jnp.concatenate([block[:, :, 1:], span_high], axis=2),
        jnp.concatenate([span_low, block[:, :, :-1]], axis=2),
    )


def stencil_kernel(
    j_ref, c_ref, cu_ref, cd_ref, low_ref, high_ref, su_ref, sd_ref, prev_ref, rate_ref, inlet_ref,
    out_ref, first_ref, last_ref, top_ref, bottom_ref, inlet_scr,
):
    span, axial = inlet_scr.shape[1:]
    for g in range(NF):
        row = inlet_ref[0, g : g + 1, :]
        inlet_scr[g] = jnp.transpose(jnp.broadcast_to(row, (axial, span)))
    lane = lax.broadcasted_iota(jnp.int32, (8, 128), 1)
    probe = pltpu.roll(lane, 1, 1)
    numpy_order = probe == (lane + 127) % 128

    at_bottom = pl.program_id(0) == 0
    at_top = pl.program_id(0) == pl.num_programs(0) - 1

    def chunk(i, carry):
        rows = pl.ds(pl.multiple_of(i * 8, 8), 8)
        cur = [c_ref[g, 0, rows, :] for g in range(NF)]
        cu = [jnp.where(at_top, high_ref[g, 0, rows, :], cu_ref[g, 0, rows, :]) for g in range(NF)]
        cd = [jnp.where(at_bottom, low_ref[g, 0, rows, :], cd_ref[g, 0, rows, :]) for g in range(NF)]
        su = [su_ref[g, 0, rows, :] for g in range(NF)]
        sd = [sd_ref[g, 0, rows, :] for g in range(NF)]
        au, ad = [], []
        for g in range(NF):
            one = pltpu.roll(cur[g], 1, 1)
            other = pltpu.roll(cur[g], 127, 1)
            down = jnp.where(numpy_order, one, other)
            up = jnp.where(numpy_order, other, one)
            ad.append(jnp.where(lane == 0, inlet_scr[g, rows, :], down))
            au.append(jnp.where(lane == 127, 0.0, up))
        dc = [cu[g] - cd[g] for g in range(NF)]
        ds = [su[g] - sd[g] for g in range(NF)]
        da = [au[g] - ad[g] for g in range(NF)]
        rate = rate_ref[0, rows, :]
        for f in range(NF):
            convection = None
            for d, diff in enumerate((dc, ds, da)):
                term = j_ref[d * NF * NF + f * NF] * diff[0]
                for g in range(1, NF):
                    term = term + j_ref[d * NF * NF + f * NF + g] * diff[g]
                convection = term if convection is None else convection + term
            laplacian = cu[f] + cd[f] + (su[f] + sd[f]) + (au[f] + ad[f]) - 6.0 * cur[f]
            residual = (
                inv_step * (cur[f] - prev_ref[f, 0, rows, :])
                + 0.5 * convection
                - viscosity * laplacian
            )
            out_ref[f, 0, rows, :] = cur[f] - rate * residual
        return carry

    lax.fori_loop(0, c_ref.shape[2] // 8, chunk, 0)
    first_ref[...] = out_ref[:, :, 0:1, :]
    last_ref[...] = out_ref[:, :, span - 1 : span, :]

    @pl.when(pl.program_id(0) == 0)
    def _():
        top_ref[...] = out_ref[...]

    @pl.when(pl.program_id(0) == pl.num_programs(0) - 1)
    def _():
        bottom_ref[...] = out_ref[...]


def sweep(current, previous, rate_cells, inlet_rows, jacobians, parts=None):
    if parts is None:
        parts = halo_parts(current)
    circ_low, circ_high, span_low, span_high = parts
    span_up = jnp.concatenate([current[:, :, 1:], span_high], axis=2)
    span_down = jnp.concatenate([span_low, current[:, :, :-1]], axis=2)
    nf, rows, span, axial = current.shape
    block = (nf, 1, span, axial)
    spec = lambda shift: pl.BlockSpec(block, lambda t: (0, t + shift, 0, 0))
    out = pl.pallas_call(
        stencil_kernel,
        grid=(rows,),
        in_specs=[
            pl.BlockSpec(memory_space=pltpu.SMEM),
            spec(0),
            pl.BlockSpec(block, lambda t: (0, jnp.minimum(t + 1, rows - 1), 0, 0)),
            pl.BlockSpec(block, lambda t: (0, jnp.maximum(t - 1, 0), 0, 0)),
            pl.BlockSpec(block, lambda t: (0, 0, 0, 0)),
            pl.BlockSpec(block, lambda t: (0, 0, 0, 0)),
            spec(0),
            spec(0),
            spec(0),
            pl.BlockSpec((1, span, axial), lambda t: (t, 0, 0)),
            pl.BlockSpec((1, nf, span), lambda t: (t, 0, 0)),
        ],
        scratch_shapes=[pltpu.VMEM((nf, span, axial), current.dtype)],
        out_specs=[spec(0)]
        + [pl.BlockSpec((nf, 1, 1, axial), lambda t: (0, t, 0, 0))] * 2
        + [pl.BlockSpec(block, lambda t: (0, 0, 0, 0))] * 2,
        out_shape=[jax.ShapeDtypeStruct(current.shape, current.dtype)]
        + [jax.ShapeDtypeStruct((nf, rows, 1, axial), current.dtype)] * 2
        + [jax.ShapeDtypeStruct(block, current.dtype)] * 2,
    )(
        jacobians.reshape(-1), current, current, current, circ_low, circ_high,
        span_up, span_down, previous, rate_cells, inlet_rows,
    )
    out, first, last, top, bottom = out
    return out, (first, last, top, bottom)


def contract(matrix, values):
    column = lambda g: matrix[:, g].reshape((-1,) + (1,) * (values.ndim - 1))
    total = column(0) * values[0][None]
    for g in range(1, matrix.shape[1]):
        total = total + column(g) * values[g][None]
    return total


def update(current, previous, rate_cells, neighbours, jacobians):
    circ_up, circ_down, span_up, span_down, axial_up, axial_down = neighbours
    convection = contract(jacobians[0], circ_up - circ_down)
    convection = convection + contract(jacobians[1], span_up - span_down)
    convection = convection + contract(jacobians[2], axial_up - axial_down)
    laplacian = (
        circ_up + circ_down + (span_up + span_down) + (axial_up + axial_down) - 6.0 * current
    )
    residual = inv_step * (current - previous) + 0.5 * convection - viscosity * laplacian
    return current - rate_cells[None] * residual


def lateral(padded):
    return (
        padded[:, 2:, 1:-1],
        padded[:, :-2, 1:-1],
        padded[:, 1:-1, 2:],
        padded[:, 1:-1, :-2],
    )


def advance(padded, current, previous, rate_cells, jacobians):
    zero_column = jnp.zeros_like(current[..., :1])
    axial_up = jnp.concatenate([current[..., 1:], zero_column], axis=-1)
    axial_down = jnp.concatenate([zero_column, current[..., :-1]], axis=-1)
    neighbours = lateral(padded) + (axial_up, axial_down)
    return update(current, previous, rate_cells, neighbours, jacobians)


def wall_zero(field_array, width):
    span_index = lax.axis_index("span")
    span_count = lax.axis_size("span")
    length = field_array.shape[2]
    position = jnp.arange(length, dtype=jnp.int32)
    at_hub = jnp.logical_and(span_index == 0, position < width)
    at_tip = jnp.logical_and(span_index == span_count - 1, position >= length - width)
    keeping = jnp.logical_not(jnp.logical_or(at_hub, at_tip)).astype(field_array.dtype)
    keeping = keeping.reshape(1, 1, length, 1)
    return field_array * keeping


def body(
    q_old, pseudo_rate, flux_jacobians, rotor_face, offsets, owners, slots, weight_idx, weight_table
):
    circ_count = lax.axis_size("circ")
    span_count = lax.axis_size("span")
    rows_local = rotor_face.shape[1]
    total_rows = rows_local * circ_count
    copies = jnp.broadcast_to(rotor_face[None], (circ_count,) + rotor_face.shape)
    gathered = lax.all_to_all(copies, "circ", 0, 0, tiled=True)
    row_iota = jnp.arange(rows_local, dtype=jnp.int32)
    first_row = lax.axis_index("circ") * rows_local
    source_rows = (first_row + row_iota[:, None] - offsets[None, :]) % total_rows
    global_rows = jnp.arange(total_rows, dtype=jnp.int32).reshape(circ_count, rows_local)
    picks = global_rows[:, None, :, None, None] == source_rows[None, None, None]
    rotated = jnp.sum(
        jnp.where(picks, gathered[:, :, :, None, :], 0.0), axis=(0, 2)
    )
    panels = rotated.reshape(NF, rows_local, KP_DEV, PW)
    table_ids = jnp.arange(weight_table.shape[0], dtype=jnp.int32)
    weights = jnp.sum(jnp.where(weight_idx[..., None] == table_ids, weight_table, 0.0), axis=-1)
    owner_of = owners[0].reshape(-1)
    slot_of = slots[0].reshape(-1)
    weight_of = weights[0].reshape(-1)
    entries = owner_of.shape[0]
    panel_of = jnp.arange(entries, dtype=jnp.int32) // owners.shape[-1]
    earlier = jnp.tril(jnp.ones((entries, entries), dtype=bool), -1)
    position = jnp.sum(earlier & (owner_of[:, None] == owner_of[None, :]), axis=1)
    chosen = (owner_of[None, None] == jnp.arange(span_count, dtype=jnp.int32)[:, None, None]) & (
        position[None, None] == jnp.arange(CAP, dtype=jnp.int32)[None, :, None]
    )
    picked = jnp.where(chosen, weight_of, 0.0)
    selection = jnp.sum(
        picked[..., None] * (panel_of[:, None] == jnp.arange(KP_DEV, dtype=jnp.int32)), axis=2
    )
    data = jnp.einsum("opk,ftkq->opftq", selection, panels, precision=lax.Precision.HIGHEST)
    code = jnp.sum(jnp.where(chosen, slot_of + 1, 0), axis=2).astype(jnp.float32) - 1.0
    payload = jnp.concatenate(
        [data.reshape(span_count, CAP, -1), code[..., None]], axis=-1
    )
    received = lax.all_to_all(payload, "span", 0, 0, tiled=True)
    values = received[..., :-1].reshape(span_count * CAP, NF, rows_local, 1, PW)
    codes = received[..., -1].reshape(span_count * CAP, 1, 1, 1, 1)
    slot_ids = jnp.arange(KP_DEV, dtype=jnp.float32).reshape(1, 1, 1, KP_DEV, 1)
    inlet_rows = jnp.transpose(
        jnp.sum(jnp.where(codes == slot_ids, values, 0.0), axis=0), (1, 0, 2, 3)
    ).reshape(rows_local, NF, KP_DEV * PW)

    mid, mid_edges = sweep(q_old, q_old, pseudo_rate, inlet_rows, flux_jacobians)
    mid_parts = halo_parts(mid, mid_edges)
    new, _ = sweep(mid, q_old, pseudo_rate, inlet_rows, flux_jacobians, mid_parts)
    return new


def solution(mesh):
    return jax.shard_map(
        body,
        mesh=mesh,
        in_specs=(
            P(None, "circ", "span", None),
            P("circ", "span", None),
            P(),
            P(None, "circ", "span"),
            P("span"),
            P("circ", "span", None),
            P("circ", "span", None),
            P("circ", "span", None),
            P(),
        ),
        out_specs=P(None, "circ", "span", None),
        check_vma=False,
    )
```
